128 devices in a mesh: rows: 8 (over y, z_lo), pairs: 16 (over z_hi, x, core).
Axes of the slice: x: 4, y: 4, z: 4 (z_hi: 2, z_lo: 2; z = z_hi * 2 + z_lo), core: 2. Of those that a mesh axis runs over, the one named last changes fastest.
Arguments:
- unit_rows: float32 [8, 16, 192, 8192], P('rows', 'pairs'), may hold values from -6 to 6
- unit_counts: int32 [8, 16], P('rows'), may hold values from 1 to 192, 1024 in all within a row
- seating: int32 [32], replicated, may hold values from 0 to 31, each once
- channel_scale: float32 [8192], replicated, may hold values from 0.25 to 4
Outputs:
- rotated: float32 [8192, 8192], P('rows', 'pairs')
The draws below stay inside these ranges and needn't reach their ends.
Inputs may be any that keep to these rules, and one draw needn't show every extreme that they name: `unit_counts`: each row of 16 counts sums to 1024, and in each row the largest is exactly 192. `seating`: each block once.
All inputs are finite; a program needn't handle non-finite values.
Results may differ from the reference program's by a relative error of at most 0.0001.
Values sent between devices are 32-bit elements; how exact they have to be, the bound alone decides.
No kernel may reach another device: no remote copies, remote signals or barrier semaphores. Data moves between devices by JAX's collectives and lax.ppermute only.
A program may use at most 128 MiB of HBM per device.

```python
import math
import jax
import jax.numpy as jnp
import numpy as np
from jax import lax

ROWS_DEV = 1024
BLOCK = 256
ROUNDS = 2
BLOCKS = 32
COLUMNS = 8192
UNIT_CAP = 192
TOTAL_ROWS = 8192
N_ROWS = 8
N_PAIRS = 16


def block_scale(rng, dims, split, smallest, high):
    def one(position, blocks):
        heights = jax.random.uniform(jax.random.fold_in(jax.random.fold_in(rng, 6), position), (blocks,), jnp.float32, smallest / len(split), high / len(split))
        return jnp.repeat(jnp.exp(heights), dims[position] // blocks).reshape((-1,) + (1,) * (len(dims) - position - 1))

    factor_of = one(*split[0])
    for cut in split[1:]:
        factor_of = factor_of * one(*cut)
    return factor_of


def split_up(number_of, total, most, lean):
    weights = [(1 << 20) // math.isqrt(grade ** lean) + 1 for grade in range(2, number_of + 1)]
    rest, given = total - most - (number_of - 1), [1] * (number_of - 1)
    while rest > 0:
        free = [i for i in range(number_of - 1) if given[i] < most]
        whole, budget = sum([weights[i] for i in free]), rest
        for i in free:
            addition = min(most - given[i], max(1, budget * weights[i] // whole), rest)
            given[i] = given[i] + addition
            rest = rest - addition
    return np.array([most] + given)


def uneven(key, amount, total, most, slope):
    if amount == 2:
        one = jax.random.randint(key, (), max(1, total - most), min(most, total - 1) + 1)
        return jnp.stack([one, total - one])
    sizes = jnp.asarray(split_up(amount, total, most, slope), jnp.int32)
    pairs = (amount - 1) // 2
    giver, taker = sizes[1:1 + 2 * pairs:2], sizes[2:2 + 2 * pairs:2]
    margin = jnp.minimum(giver - 1, most - taker)
    shifted = jax.random.randint(jax.random.fold_in(key, 1), (pairs,), 0, 1 << 20) % (margin + 1)
    sizes = sizes.at[1:1 + 2 * pairs:2].set(giver - shifted).at[2:2 + 2 * pairs:2].set(taker + shifted)
    return sizes[jax.random.permutation(jax.random.fold_in(key, 2), amount)]


def noise(stream_key, dims, spread, most, shards=(), kind=jnp.bfloat16):
    loudness = block_scale(stream_key, dims, shards, -0.22, 0.18) if shards else 1.0
    entries = jax.random.normal(stream_key, dims, jnp.float32) * spread * loudness
    return jnp.minimum(jnp.maximum(entries, -most), most).astype(kind)


def setup_inputs(seed: int = 0) -> dict:
    streams_of = jax.random.split(jax.random.key(seed), 5)
    unit_rows = noise(streams_of[0], (N_ROWS, N_PAIRS, UNIT_CAP, COLUMNS), 1.0, 6.0, ((0, 8), (1, 16)), jnp.float32)
    unit_counts = jax.vmap(lambda own: uneven(own, N_PAIRS, ROWS_DEV, UNIT_CAP, 2))(jax.random.split(streams_of[1], N_ROWS)).reshape((N_ROWS, N_PAIRS)).astype(jnp.int32)
    seating = jax.random.permutation(streams_of[2], BLOCKS).astype(jnp.int32)
    channel_scale = jnp.clip(jnp.exp(jax.random.uniform(streams_of[3], (COLUMNS,), jnp.float32, math.log(0.25), math.log(4.0))), 0.25, 4.0)
    return {"unit_rows": unit_rows, "unit_counts": unit_counts, "seating": seating, "channel_scale": channel_scale}


epsilon = 1e-06

def rotate(pair_panel):
    gram_full = lax.dot_general(pair_panel.astype(jnp.float32), pair_panel.astype(jnp.float32), (((0,), (0,)), ((), ())), precision=lax.Precision.HIGHEST, preferred_element_type=jnp.float32)
    diag_terms = jnp.diagonal(gram_full)
    skew_part = gram_full * (diag_terms[None, :] - diag_terms[:, None]) / (2.0 * (diag_terms[:, None] ** 2 + diag_terms[None, :] ** 2) + epsilon)
    skew_square = jnp.dot(skew_part, skew_part, precision=lax.Precision.HIGHEST)
    identity = jnp.eye(skew_part.shape[0], dtype=jnp.float32)
    numerator = identity + skew_part + 0.25 * skew_square
    sym_part = identity - 0.25 * skew_square
    rotation = jnp.linalg.solve(sym_part, numerator.T).T
    return jnp.dot(pair_panel, rotation, precision=lax.Precision.HIGHEST)

def advance(seated):
    upper = seated[:, 0::2]
    lower = seated[:, 1::2]
    new_upper = jnp.concatenate([upper[:, :1], lower[:, :1], upper[:, 1:-1]], axis=1)
    new_lower = jnp.concatenate([lower[:, 1:], upper[:, -1:]], axis=1)
    return jnp.stack([new_upper, new_lower], axis=2).reshape(seated.shape)

def reference(unit_rows, unit_counts, seating, channel_scale):
    flat_rows = unit_rows.reshape(N_ROWS * N_PAIRS * UNIT_CAP, COLUMNS)
    flat_counts = unit_counts.reshape(N_ROWS * N_PAIRS).astype(jnp.int32)
    unit_ends = jnp.cumsum(flat_counts).astype(jnp.int32)
    target = jnp.arange(TOTAL_ROWS, dtype=jnp.int32)
    passed = (target[:, None] >= unit_ends[None, :]).astype(jnp.int32)
    owner_unit = jnp.sum(passed, axis=1).astype(jnp.int32)
    owner_start = jnp.sum(passed * flat_counts[None, :], axis=1).astype(jnp.int32)
    source = (owner_unit * UNIT_CAP + target - owner_start).astype(jnp.int32)
    residuals = jnp.take(flat_rows, source, axis=0) * channel_scale[None, :]
    seated = jnp.take(residuals.reshape(TOTAL_ROWS, BLOCKS, BLOCK), seating.astype(jnp.int32), axis=1)
    for round_index in range(ROUNDS):
        pair_panels = seated.reshape(TOTAL_ROWS, N_PAIRS, 2 * BLOCK).transpose(1, 0, 2)
        turned = lax.map(rotate, pair_panels)
        seated = turned.transpose(1, 0, 2).reshape(TOTAL_ROWS, BLOCKS, BLOCK)
        if round_index + 1 < ROUNDS:
            seated = advance(seated)
    return seated.reshape(TOTAL_ROWS, COLUMNS)
```

```python
import jax
import jax.numpy as jnp
from jax import lax
from jax.sharding import PartitionSpec as P

ROWS_DEV = 1024
BLOCK = 256
ROUNDS = 2

epsilon = 1e-06
HI = lax.Precision.HIGHEST
NEWTON_TOL_SQ = 1e-4
NEWTON_MAX = 60


def passed_along(array, axis, by):
    length = lax.axis_size(axis)
    pairs = [(i, i + by) for i in range(length) if 0 <= i + by < length]
    return lax.ppermute(array, axis, pairs)


def spd_inverse(sym_part):
    n = sym_part.shape[0]
    identity = jnp.eye(n, dtype=jnp.float32)
    bound = jnp.max(jnp.sum(jnp.abs(sym_part), axis=1))
    scale = 2.0 / (1.0 + bound)
    inverse = scale * identity
    residual = identity - scale * sym_part

    def cond(state):
        step, _, _, err = state
        return jnp.logical_and(err > NEWTON_TOL_SQ, step < NEWTON_MAX)

    def body(state):
        step, inverse, residual, _ = state
        inverse = inverse + jnp.dot(inverse, residual, precision=HI)
        residual = identity - jnp.dot(sym_part, inverse, precision=HI)
        return step + 1, inverse, residual, jnp.sum(residual * residual)

    state = (jnp.int32(0), inverse, residual, jnp.sum(residual * residual))
    _, inverse, residual, _ = lax.while_loop(cond, body, state)
    inverse = inverse + jnp.dot(inverse, residual, precision=HI)
    residual = identity - jnp.dot(sym_part, inverse, precision=HI)
    inverse = inverse + jnp.dot(inverse, residual, precision=HI)
    return inverse


def rotate(panels):
    partial_gram = lax.dot_general(
        panels,
        panels,
        (((0,), (0,)), ((), ())),
        precision=HI,
        preferred_element_type=jnp.float32,
    )
    gram_full = lax.psum(partial_gram, "rows")
    diag_terms = jnp.diagonal(gram_full)
    skew_part = (
        gram_full
        * (diag_terms[None, :] - diag_terms[:, None])
        / (2.0 * (diag_terms[:, None] ** 2 + diag_terms[None, :] ** 2) + epsilon)
    )
    skew_square = jnp.dot(skew_part, skew_part, precision=HI)
    identity = jnp.eye(skew_part.shape[0], dtype=jnp.float32)
    numerator = identity + skew_part + 0.25 * skew_square
    sym_part = identity - 0.25 * skew_square
    rotation = jnp.dot(numerator, spd_inverse(sym_part), precision=HI)
    return jnp.dot(panels, rotation, precision=HI)


def advance(panels):
    half_width = panels.shape[1] // 2
    upper = panels[:, :half_width]
    lower = panels[:, half_width:]
    pair_index = lax.axis_index("pairs")
    last_pair = lax.axis_size("pairs") - 1
    upward = jnp.where(pair_index == 0, lower, upper)
    came_up = passed_along(upward, "pairs", 1)
    came_down = passed_along(lower, "pairs", -1)
    new_upper = jnp.where(pair_index == 0, upper, came_up)
    new_lower = jnp.where(pair_index == last_pair, upper, came_down)
    return jnp.concatenate([new_upper, new_lower], axis=1)


def compact(panels, group_counts, capacity):
    unit_ends = jnp.cumsum(group_counts)
    target = lax.iota(jnp.int32, ROWS_DEV)
    passed = (target[:, None] >= unit_ends[None, :]).astype(jnp.int32)
    owner_unit = jnp.sum(passed, axis=1)
    owner_start = jnp.sum(passed * group_counts[None, :], axis=1)
    source = owner_unit * capacity + target - owner_start
    return jnp.take(panels, source, axis=0)


def local(unit_rows, unit_counts, seating, channel_scale):
    capacity = unit_rows.shape[2]
    columns = unit_rows.shape[3]
    group_counts = unit_counts[0]
    scaled = unit_rows[0, 0] * channel_scale[None, :]
    seated = jnp.take(scaled.reshape(capacity, columns // BLOCK, BLOCK), seating, axis=1).reshape(
        capacity, columns
    )
    panels = lax.all_to_all(seated, "pairs", split_axis=1, concat_axis=0, tiled=True)
    current = compact(panels, group_counts, capacity)
    for round_index in range(ROUNDS):
        current = rotate(current)
        if round_index + 1 < ROUNDS:
            current = advance(current)
    return current


def solution(mesh):
    return jax.shard_map(
        local,
        mesh=mesh,
        in_specs=(P("rows", "pairs", None, None), P("rows", None), P(), P()),
        out_specs=P("rows", "pairs"),
        check_vma=False,
    )
```

```python
import jax
import jax.numpy as jnp
from jax import lax
from jax.experimental import pallas as pl
from jax.experimental.pallas import tpu as pltpu
from jax.sharding import PartitionSpec as P

ROWS_DEV = 1024
BLOCK = 256
ROUNDS = 2

epsilon = 1e-06
HI = lax.Precision.HIGHEST
NEWTON_TOL_SQ = 1e-4
NEWTON_MAX = 60


def passed_along(array, axis, by):
    length = lax.axis_size(axis)
    pairs = [(i, i + by) for i in range(length) if 0 <= i + by < length]
    return lax.ppermute(array, axis, pairs)


def spd_inverse(sym_part):
    n = sym_part.shape[0]
    identity = jnp.eye(n, dtype=jnp.float32)
    bound = jnp.max(jnp.sum(jnp.abs(sym_part), axis=1))
    scale = 2.0 / (1.0 + bound)
    inverse = scale * identity
    residual = identity - scale * sym_part

    def cond(state):
        step, _, _, err = state
        return jnp.logical_and(err > NEWTON_TOL_SQ, step < NEWTON_MAX)

    def body(state):
        step, inverse, residual, _ = state
        inverse = inverse + jnp.dot(inverse, residual, precision=HI)
        residual = identity - jnp.dot(sym_part, inverse, precision=HI)
        return step + 1, inverse, residual, jnp.sum(residual * residual)

    state = (jnp.int32(0), inverse, residual, jnp.sum(residual * residual))
    _, inverse, residual, _ = lax.while_loop(cond, body, state)
    inverse = inverse + jnp.dot(inverse, residual, precision=HI)
    residual = identity - jnp.dot(sym_part, inverse, precision=HI)
    inverse = inverse + jnp.dot(inverse, residual, precision=HI)
    return inverse


def row_sum(partial, axis):
    count = lax.axis_size(axis)
    rows, cols = partial.shape
    pieces = lax.all_to_all(partial.reshape(count, rows // count, cols), axis, 0, 0, tiled=False)
    block = jnp.sum(pieces, axis=0)
    spread = jnp.broadcast_to(block[None], (count, rows // count, cols))
    return lax.all_to_all(spread, axis, 0, 0, tiled=False).reshape(rows, cols)


def seat_kernel(seat_ref, upper_ref, lower_ref, upper_scale, lower_scale, out_ref):
    out_ref[0, :, :BLOCK] = upper_ref[...] * upper_scale[...]
    out_ref[0, :, BLOCK:] = lower_ref[...] * lower_scale[...]


def seat_and_scale(rows, scale, seating):
    capacity, columns = rows.shape
    pairs = columns // (2 * BLOCK)
    block_of = lambda half: (lambda q, seat: (0, seat[2 * q + half]))
    return pl.pallas_call(
        seat_kernel,
        out_shape=jax.ShapeDtypeStruct((pairs, capacity, 2 * BLOCK), jnp.float32),
        grid_spec=pltpu.PrefetchScalarGridSpec(
            num_scalar_prefetch=1,
            grid=(pairs,),
            in_specs=[
                pl.BlockSpec((capacity, BLOCK), block_of(0)),
                pl.BlockSpec((capacity, BLOCK), block_of(1)),
                pl.BlockSpec((1, BLOCK), block_of(0)),
                pl.BlockSpec((1, BLOCK), block_of(1)),
            ],
            out_specs=pl.BlockSpec((1, capacity, 2 * BLOCK), lambda q, seat: (q, 0, 0)),
        ),
    )(seating, rows, rows, scale.reshape(1, columns), scale.reshape(1, columns))


def rotate(panels):
    partial_gram = lax.dot_general(
        panels,
        panels,
        (((0,), (0,)), ((), ())),
        precision=HI,
        preferred_element_type=jnp.float32,
    )
    gram_full = row_sum(partial_gram, "rows")
    identity = jnp.eye(gram_full.shape[0], dtype=jnp.float32)
    diag_terms = jnp.sum(gram_full * identity, axis=0)
    skew_part = (
        gram_full
        * (diag_terms[None, :] - diag_terms[:, None])
        / (2.0 * (diag_terms[:, None] ** 2 + diag_terms[None, :] ** 2) + epsilon)
    )
    skew_square = jnp.dot(skew_part, skew_part, precision=HI)
    numerator = identity + skew_part + 0.25 * skew_square
    sym_part = identity - 0.25 * skew_square
    rotation = jnp.dot(numerator, spd_inverse(sym_part), precision=HI)
    return jnp.dot(panels, rotation, precision=HI)


def advance(panels):
    half_width = panels.shape[1] // 2
    upper = panels[:, :half_width]
    lower = panels[:, half_width:]
    pair_index = lax.axis_index("pairs")
    last_pair = lax.axis_size("pairs") - 1
    upward = jnp.where(pair_index == 0, lower, upper)
    came_up = passed_along(upward, "pairs", 1)
    came_down = passed_along(lower, "pairs", -1)
    new_upper = jnp.where(pair_index == 0, upper, came_up)
    new_lower = jnp.where(pair_index == last_pair, upper, came_down)
    return jnp.concatenate([new_upper, new_lower], axis=1)


def compact(panels, group_counts, capacity):
    unit_ends = jnp.cumsum(group_counts)
    target = lax.iota(jnp.int32, ROWS_DEV)
    passed = (target[:, None] >= unit_ends[None, :]).astype(jnp.int32)
    owner_unit = jnp.sum(passed, axis=1)
    owner_start = jnp.sum(passed * group_counts[None, :], axis=1)
    source = owner_unit * capacity + target - owner_start
    return jnp.take(panels, source, axis=0, mode="clip")


def local(unit_rows, unit_counts, seating, channel_scale):
    capacity = unit_rows.shape[2]
    group_counts = unit_counts[0]
    seated = seat_and_scale(unit_rows[0, 0], channel_scale, seating)
    panels = lax.all_to_all(seated, "pairs", 0, 0, tiled=True)
    current = compact(panels.reshape(-1, 2 * BLOCK), group_counts, capacity)
    for round_index in range(ROUNDS):
        current = rotate(current)
        if round_index + 1 < ROUNDS:
            current = advance(current)
    return current


def solution(mesh):
    return jax.shard_map(
        local,
        mesh=mesh,
        in_specs=(P("rows", "pairs", None, None), P("rows", None), P(), P()),
        out_specs=P("rows", "pairs"),
        check_vma=False,
    )
```

```python
import jax
import jax.numpy as jnp
from jax import lax
from jax.experimental import pallas as pl
from jax.experimental.pallas import tpu as pltpu
from jax.sharding import PartitionSpec as P

ROWS_DEV = 1024
BLOCK = 256


epsilon = 1e-06
HI = lax.Precision.HIGHEST
NEWTON_TOL_SQ = 1e-4
NEWTON_MAX = 60


def passed_along(array, axis, by):
    length = lax.axis_size(axis)
    pairs = [(i, i + by) for i in range(length) if 0 <= i + by < length]
    return lax.ppermute(array, axis, pairs)


def spd_inverse(sym_part):
    n = sym_part.shape[0]
    identity = jnp.eye(n, dtype=jnp.float32)
    bound = jnp.max(jnp.sum(jnp.abs(sym_part), axis=1))
    scale = 2.0 / (1.0 + bound)
    inverse = scale * identity
    residual = identity - scale * sym_part

    def cond(state):
        step, _, _, err = state
        return jnp.logical_and(err > NEWTON_TOL_SQ, step < NEWTON_MAX)

    def body(state):
        step, inverse, residual, _ = state
        inverse = inverse + jnp.dot(inverse, residual, precision=HI)
        residual = identity - jnp.dot(sym_part, inverse, precision=HI)
        return step + 1, inverse, residual, jnp.sum(residual * residual)

    state = (jnp.int32(0), inverse, residual, jnp.sum(residual * residual))
    _, inverse, residual, _ = lax.while_loop(cond, body, state)
    inverse = inverse + jnp.dot(inverse, residual, precision=HI)
    residual = identity - jnp.dot(sym_part, inverse, precision=HI)
    inverse = inverse + jnp.dot(inverse, residual, precision=HI)
    return inverse


def row_sum(partial, axis):
    count = lax.axis_size(axis)
    rows, cols = partial.shape
    pieces = lax.all_to_all(partial.reshape(count, rows // count, cols), axis, 0, 0, tiled=False)
    block = jnp.sum(pieces, axis=0)
    spread = jnp.broadcast_to(block[None], (count, rows // count, cols))
    return lax.all_to_all(spread, axis, 0, 0, tiled=False).reshape(rows, cols)


def seat_kernel(seat_ref, upper_ref, lower_ref, upper_scale, lower_scale, out_ref):
    out_ref[0, :, :BLOCK] = upper_ref[...] * upper_scale[...]
    out_ref[0, :, BLOCK:] = lower_ref[...] * lower_scale[...]


def seat_and_scale(rows, scale, seating):
    capacity, columns = rows.shape
    pairs = columns // (2 * BLOCK)
    block_of = lambda half: (lambda q, seat: (0, seat[2 * q + half]))
    return pl.pallas_call(
        seat_kernel,
        out_shape=jax.ShapeDtypeStruct((pairs, capacity, 2 * BLOCK), jnp.float32),
        grid_spec=pltpu.PrefetchScalarGridSpec(
            num_scalar_prefetch=1,
            grid=(pairs,),
            in_specs=[
                pl.BlockSpec((capacity, BLOCK), block_of(0)),
                pl.BlockSpec((capacity, BLOCK), block_of(1)),
                pl.BlockSpec((1, BLOCK), block_of(0)),
                pl.BlockSpec((1, BLOCK), block_of(1)),
            ],
            out_specs=pl.BlockSpec((1, capacity, 2 * BLOCK), lambda q, seat: (q, 0, 0)),
        ),
    )(seating, rows, rows, scale.reshape(1, columns), scale.reshape(1, columns))


def row_gather_sum(partial, axis):
    count = lax.axis_size(axis)
    spread = jnp.broadcast_to(partial[None], (count,) + partial.shape)
    return jnp.sum(lax.all_to_all(spread, axis, 0, 0, tiled=False), axis=0)


def cayley(gram_full):
    identity = jnp.eye(gram_full.shape[0], dtype=jnp.float32)
    diag_terms = jnp.sum(gram_full * identity, axis=0)
    skew_part = (
        gram_full
        * (diag_terms[None, :] - diag_terms[:, None])
        / (2.0 * (diag_terms[:, None] ** 2 + diag_terms[None, :] ** 2) + epsilon)
    )
    skew_square = jnp.dot(skew_part, skew_part, precision=HI)
    numerator = identity + skew_part + 0.25 * skew_square
    sym_part = identity - 0.25 * skew_square
    return jnp.dot(numerator, spd_inverse(sym_part), precision=HI)


def first_round(panels):
    partial_gram = lax.dot_general(
        panels,
        panels,
        (((0,), (0,)), ((), ())),
        precision=HI,
        preferred_element_type=jnp.float32,
    )
    gram_full = row_sum(partial_gram, "rows")
    rotation = cayley(gram_full)
    turned = jnp.dot(panels, rotation, precision=HI)
    turned_gram = lax.dot_general(
        rotation,
        jnp.dot(gram_full, rotation, precision=HI),
        (((0,), (0,)), ((), ())),
        precision=HI,
    )
    return turned, turned_gram


def advance(panels, gram):
    half_width = panels.shape[1] // 2
    rows = panels.shape[0]
    upper = panels[:, :half_width]
    lower = panels[:, half_width:]
    upper_gram = gram[:half_width, :half_width]
    lower_gram = gram[half_width:, half_width:]
    pair_index = lax.axis_index("pairs")
    last_pair = lax.axis_size("pairs") - 1
    first = pair_index == 0
    last = pair_index == last_pair
    upward = jnp.concatenate(
        [jnp.where(first, lower, upper), jnp.where(first, lower_gram, upper_gram)], axis=0
    )
    came_up = passed_along(upward, "pairs", 1)
    came_down = passed_along(jnp.concatenate([lower, lower_gram], axis=0), "pairs", -1)
    new_upper = jnp.where(first, upper, came_up[:rows])
    new_upper_gram = jnp.where(first, upper_gram, came_up[rows:])
    new_lower = jnp.where(last, upper, came_down[:rows])
    new_lower_gram = jnp.where(last, upper_gram, came_down[rows:])
    return new_upper, new_lower, new_upper_gram, new_lower_gram


def second_round(upper, lower, upper_gram, lower_gram):
    partial_cross = lax.dot_general(
        upper,
        lower,
        (((0,), (0,)), ((), ())),
        precision=HI,
        preferred_element_type=jnp.float32,
    )
    cross = row_gather_sum(partial_cross, "rows")
    gram_full = jnp.concatenate(
        [
            jnp.concatenate([upper_gram, cross], axis=1),
            jnp.concatenate([cross.T, lower_gram], axis=1),
        ],
        axis=0,
    )
    rotation = cayley(gram_full)
    half_width = upper.shape[1]
    return jnp.dot(upper, rotation[:half_width], precision=HI) + jnp.dot(
        lower, rotation[half_width:], precision=HI
    )


def compact(panels, group_counts, capacity):
    unit_ends = jnp.cumsum(group_counts)
    target = lax.iota(jnp.int32, ROWS_DEV)
    passed = (target[:, None] >= unit_ends[None, :]).astype(jnp.int32)
    owner_unit = jnp.sum(passed, axis=1)
    owner_start = jnp.sum(passed * group_counts[None, :], axis=1)
    source = owner_unit * capacity + target - owner_start
    return jnp.take(panels, source, axis=0, mode="clip")


def local(unit_rows, unit_counts, seating, channel_scale):
    capacity = unit_rows.shape[2]
    group_counts = unit_counts[0]
    seated = seat_and_scale(unit_rows[0, 0], channel_scale, seating)
    panels = lax.all_to_all(seated, "pairs", 0, 0, tiled=True)
    current = compact(panels.reshape(-1, 2 * BLOCK), group_counts, capacity)
    turned, turned_gram = first_round(current)
    return second_round(*advance(turned, turned_gram))


def solution(mesh):
    return jax.shard_map(
        local,
        mesh=mesh,
        in_specs=(P("rows", "pairs", None, None), P("rows", None), P(), P()),
        out_specs=P("rows", "pairs"),
        check_vma=False,
    )
```

```python
import jax
import jax.numpy as jnp
from jax import lax
from jax.experimental import pallas as pl
from jax.experimental.pallas import tpu as pltpu
from jax.sharding import PartitionSpec as P

ROWS_DEV = 1024
BLOCK = 256


epsilon = 1e-06
HI = lax.Precision.HIGHEST
NEWTON_TOL_SQ = 1e-6
NEWTON_MAX = 60


def passed_along(array, axis, by):
    length = lax.axis_size(axis)
    pairs = [(i, i + by) for i in range(length) if 0 <= i + by < length]
    return lax.ppermute(array, axis, pairs)


def spd_inverse(sym_part):
    n = sym_part.shape[0]
    identity = jnp.eye(n, dtype=jnp.float32)
    bound = jnp.max(jnp.sum(jnp.abs(sym_part), axis=1))
    scale = 2.0 / (1.0 + bound)
    inverse = scale * identity
    residual = identity - scale * sym_part

    def cond(state):
        step, _, _, err = state
        return jnp.logical_and(err > NEWTON_TOL_SQ, step < NEWTON_MAX)

    def body(state):
        step, inverse, residual, _ = state
        inverse = inverse + jnp.dot(inverse, residual, precision=HI)
        residual = identity - jnp.dot(sym_part, inverse, precision=HI)
        return step + 1, inverse, residual, jnp.sum(residual * residual)

    state = (jnp.int32(0), inverse, residual, jnp.sum(residual * residual))
    _, inverse, residual, _ = lax.while_loop(cond, body, state)
    return inverse + jnp.dot(inverse, residual, precision=HI)


def row_sum(partial, axis):
    count = lax.axis_size(axis)
    rows, cols = partial.shape
    pieces = lax.all_to_all(partial.reshape(count, rows // count, cols), axis, 0, 0, tiled=False)
    block = jnp.sum(pieces, axis=0)
    spread = jnp.broadcast_to(block[None], (count, rows // count, cols))
    return lax.all_to_all(spread, axis, 0, 0, tiled=False).reshape(rows, cols)


def seat_kernel(seat_ref, *refs):
    count = (len(refs) - 1) // 2
    blocks, scales, out_ref = refs[:count], refs[count:2 * count], refs[-1]
    for k in range(count):
        out_ref[k // 2, :, (k % 2) * BLOCK:(k % 2 + 1) * BLOCK] = blocks[k][...] * scales[k][...]


def seat_and_scale(rows, scale, seating):
    capacity, columns = rows.shape
    pairs = columns // (2 * BLOCK)
    step_pairs = 4
    seats = 2 * step_pairs
    block_of = lambda k: (lambda q, seat: (0, seat[seats * q + k]))
    return pl.pallas_call(
        seat_kernel,
        out_shape=jax.ShapeDtypeStruct((pairs, capacity, 2 * BLOCK), jnp.float32),
        grid_spec=pltpu.PrefetchScalarGridSpec(
            num_scalar_prefetch=1,
            grid=(pairs // step_pairs,),
            in_specs=[pl.BlockSpec((capacity, BLOCK), block_of(k)) for k in range(seats)]
            + [pl.BlockSpec((1, BLOCK), block_of(k)) for k in range(seats)],
            out_specs=pl.BlockSpec((step_pairs, capacity, 2 * BLOCK), lambda q, seat: (q, 0, 0)),
        ),
    )(seating, *([rows] * seats), *([scale.reshape(1, columns)] * seats))


def row_gather_sum(partial, axis):
    count = lax.axis_size(axis)
    spread = jnp.broadcast_to(partial[None], (count,) + partial.shape)
    return jnp.sum(lax.all_to_all(spread, axis, 0, 0, tiled=False), axis=0)


def cayley(gram_full):
    identity = jnp.eye(gram_full.shape[0], dtype=jnp.float32)
    diag_terms = jnp.sum(gram_full * identity, axis=0)
    skew_part = (
        gram_full
        * (diag_terms[None, :] - diag_terms[:, None])
        / (2.0 * (diag_terms[:, None] ** 2 + diag_terms[None, :] ** 2) + epsilon)
    )
    skew_square = jnp.dot(skew_part, skew_part, precision=HI)
    numerator = identity + skew_part + 0.25 * skew_square
    sym_part = identity - 0.25 * skew_square
    return jnp.dot(numerator, spd_inverse(sym_part), precision=HI)


def first_round(panels):
    partial_gram = lax.dot_general(
        panels,
        panels,
        (((0,), (0,)), ((), ())),
        precision=HI,
        preferred_element_type=jnp.float32,
    )
    gram_full = row_sum(partial_gram, "rows")
    rotation = cayley(gram_full)
    turned = jnp.dot(panels, rotation, precision=HI)
    gram_turned = jnp.dot(gram_full, rotation, precision=HI)
    half_width = panels.shape[1] // 2
    block_gram = lambda cut: lax.dot_general(
        rotation[:, cut], gram_turned[:, cut], (((0,), (0,)), ((), ())), precision=HI
    )
    return turned, block_gram(slice(0, half_width)), block_gram(slice(half_width, None))


def advance(panels, upper_gram, lower_gram):
    half_width = panels.shape[1] // 2
    rows = panels.shape[0]
    upper = panels[:, :half_width]
    lower = panels[:, half_width:]
    pair_index = lax.axis_index("pairs")
    last_pair = lax.axis_size("pairs") - 1
    first = pair_index == 0
    last = pair_index == last_pair
    upward = jnp.concatenate(
        [jnp.where(first, lower, upper), jnp.where(first, lower_gram, upper_gram)], axis=0
    )
    came_up = passed_along(upward, "pairs", 1)
    came_down = passed_along(jnp.concatenate([lower, lower_gram], axis=0), "pairs", -1)
    new_upper = jnp.where(first, upper, came_up[:rows])
    new_upper_gram = jnp.where(first, upper_gram, came_up[rows:])
    new_lower = jnp.where(last, upper, came_down[:rows])
    new_lower_gram = jnp.where(last, upper_gram, came_down[rows:])
    return new_upper, new_lower, new_upper_gram, new_lower_gram


def second_round(upper, lower, upper_gram, lower_gram):
    partial_cross = lax.dot_general(
        upper,
        lower,
        (((0,), (0,)), ((), ())),
        precision=HI,
        preferred_element_type=jnp.float32,
    )
    cross = row_gather_sum(partial_cross, "rows")
    gram_full = jnp.concatenate(
        [
            jnp.concatenate([upper_gram, cross], axis=1),
            jnp.concatenate([cross.T, lower_gram], axis=1),
        ],
        axis=0,
    )
    rotation = cayley(gram_full)
    half_width = upper.shape[1]
    return jnp.dot(upper, rotation[:half_width], precision=HI) + jnp.dot(
        lower, rotation[half_width:], precision=HI
    )


def compact(panels, group_counts, capacity):
    unit_ends = jnp.cumsum(group_counts)
    target = lax.iota(jnp.int32, ROWS_DEV)
    passed = (target[:, None] >= unit_ends[None, :]).astype(jnp.int32)
    owner_unit = jnp.sum(passed, axis=1)
    owner_start = jnp.sum(passed * group_counts[None, :], axis=1)
    source = owner_unit * capacity + target - owner_start
    return jnp.take(panels, source, axis=0, mode="clip")


def local(unit_rows, unit_counts, seating, channel_scale):
    capacity = unit_rows.shape[2]
    group_counts = unit_counts[0]
    seated = seat_and_scale(unit_rows[0, 0], channel_scale, seating)
    panels = lax.all_to_all(seated, "pairs", 0, 0, tiled=True)
    current = compact(panels.reshape(-1, 2 * BLOCK), group_counts, capacity)
    return second_round(*advance(*first_round(current)))


def solution(mesh):
    return jax.shard_map(
        local,
        mesh=mesh,
        in_specs=(P("rows", "pairs", None, None), P("rows", None), P(), P()),
        out_specs=P("rows", "pairs"),
        check_vma=False,
    )
```

```python
import jax
import jax.numpy as jnp
from jax import lax
from jax.experimental import pallas as pl
from jax.experimental.pallas import tpu as pltpu
from jax.sharding import PartitionSpec as P

ROWS_DEV = 1024
BLOCK = 256


epsilon = 1e-06
HI = lax.Precision.HIGHEST
BIG = lax.Precision.HIGH
NEWTON_TOL_SQ = 1e-6
NEWTON_MAX = 60


def passed_along(array, axis, by):
    length = lax.axis_size(axis)
    pairs = [(i, i + by) for i in range(length) if 0 <= i + by < length]
    return lax.ppermute(array, axis, pairs)


def spd_inverse(sym_part):
    n = sym_part.shape[0]
    identity = jnp.eye(n, dtype=jnp.float32)
    bound = jnp.max(jnp.sum(jnp.abs(sym_part), axis=1))
    scale = 2.0 / (1.0 + bound)
    inverse = scale * identity
    residual = identity - scale * sym_part

    def cond(state):
        step, _, _, err = state
        return jnp.logical_and(err > NEWTON_TOL_SQ, step < NEWTON_MAX)

    def body(state):
        step, inverse, residual, _ = state
        inverse = inverse + jnp.dot(inverse, residual, precision=HI)
        residual = identity - jnp.dot(sym_part, inverse, precision=HI)
        return step + 1, inverse, residual, jnp.sum(residual * residual)

    state = (jnp.int32(0), inverse, residual, jnp.sum(residual * residual))
    _, inverse, residual, _ = lax.while_loop(cond, body, state)
    return inverse + jnp.dot(inverse, residual, precision=HI)


def row_sum(partial, axis):
    count = lax.axis_size(axis)
    rows, cols = partial.shape
    pieces = lax.all_to_all(partial.reshape(count, rows // count, cols), axis, 0, 0, tiled=False)
    block = jnp.sum(pieces, axis=0)
    spread = jnp.broadcast_to(block[None], (count, rows // count, cols))
    return lax.all_to_all(spread, axis, 0, 0, tiled=False).reshape(rows, cols)


def seat_kernel(seat_ref, *refs):
    count = (len(refs) - 1) // 2
    blocks, scales, out_ref = refs[:count], refs[count:2 * count], refs[-1]
    for k in range(count):
        out_ref[k // 2, :, (k % 2) * BLOCK:(k % 2 + 1) * BLOCK] = blocks[k][...] * scales[k][...]


def seat_and_scale(rows, scale, seating):
    capacity, columns = rows.shape
    pairs = columns // (2 * BLOCK)
    step_pairs = 4
    seats = 2 * step_pairs
    block_of = lambda k: (lambda q, seat: (0, seat[seats * q + k]))
    return pl.pallas_call(
        seat_kernel,
        out_shape=jax.ShapeDtypeStruct((pairs, capacity, 2 * BLOCK), jnp.float32),
        grid_spec=pltpu.PrefetchScalarGridSpec(
            num_scalar_prefetch=1,
            grid=(pairs // step_pairs,),
            in_specs=[pl.BlockSpec((capacity, BLOCK), block_of(k)) for k in range(seats)]
            + [pl.BlockSpec((1, BLOCK), block_of(k)) for k in range(seats)],
            out_specs=pl.BlockSpec((step_pairs, capacity, 2 * BLOCK), lambda q, seat: (q, 0, 0)),
        ),
    )(seating, *([rows] * seats), *([scale.reshape(1, columns)] * seats))


def row_gather_sum(partial, axis):
    count = lax.axis_size(axis)
    spread = jnp.broadcast_to(partial[None], (count,) + partial.shape)
    return jnp.sum(lax.all_to_all(spread, axis, 0, 0, tiled=False), axis=0)


def cayley(gram_full):
    identity = jnp.eye(gram_full.shape[0], dtype=jnp.float32)
    diag_terms = jnp.sum(gram_full * identity, axis=0)
    skew_part = (
        gram_full
        * (diag_terms[None, :] - diag_terms[:, None])
        / (2.0 * (diag_terms[:, None] ** 2 + diag_terms[None, :] ** 2) + epsilon)
    )
    skew_square = jnp.dot(skew_part, skew_part, precision=HI)
    numerator = identity + skew_part + 0.25 * skew_square
    sym_part = identity - 0.25 * skew_square
    return jnp.dot(numerator, spd_inverse(sym_part), precision=HI)


def first_round(panels):
    partial_gram = lax.dot_general(
        panels,
        panels,
        (((0,), (0,)), ((), ())),
        precision=BIG,
        preferred_element_type=jnp.float32,
    )
    gram_full = row_sum(partial_gram, "rows")
    rotation = cayley(gram_full)
    turned = jnp.dot(panels, rotation, precision=BIG)
    gram_turned = jnp.dot(gram_full, rotation, precision=HI)
    half_width = panels.shape[1] // 2
    block_gram = lambda cut: lax.dot_general(
        rotation[:, cut], gram_turned[:, cut], (((0,), (0,)), ((), ())), precision=HI
    )
    return turned, block_gram(slice(0, half_width)), block_gram(slice(half_width, None))


def advance(panels, upper_gram, lower_gram):
    half_width = panels.shape[1] // 2
    rows = panels.shape[0]
    upper = panels[:, :half_width]
    lower = panels[:, half_width:]
    pair_index = lax.axis_index("pairs")
    last_pair = lax.axis_size("pairs") - 1
    first = pair_index == 0
    last = pair_index == last_pair
    upward = jnp.concatenate(
        [jnp.where(first, lower, upper), jnp.where(first, lower_gram, upper_gram)], axis=0
    )
    came_up = passed_along(upward, "pairs", 1)
    came_down = passed_along(jnp.concatenate([lower, lower_gram], axis=0), "pairs", -1)
    new_upper = jnp.where(first, upper, came_up[:rows])
    new_upper_gram = jnp.where(first, upper_gram, came_up[rows:])
    new_lower = jnp.where(last, upper, came_down[:rows])
    new_lower_gram = jnp.where(last, upper_gram, came_down[rows:])
    return new_upper, new_lower, new_upper_gram, new_lower_gram


def second_round(upper, lower, upper_gram, lower_gram):
    partial_cross = lax.dot_general(
        upper,
        lower,
        (((0,), (0,)), ((), ())),
        precision=BIG,
        preferred_element_type=jnp.float32,
    )
    cross = row_gather_sum(partial_cross, "rows")
    gram_full = jnp.concatenate(
        [
            jnp.concatenate([upper_gram, cross], axis=1),
            jnp.concatenate([cross.T, lower_gram], axis=1),
        ],
        axis=0,
    )
    rotation = cayley(gram_full)
    half_width = upper.shape[1]
    return jnp.dot(upper, rotation[:half_width], precision=BIG) + jnp.dot(
        lower, rotation[half_width:], precision=BIG
    )


def compact(panels, group_counts, capacity):
    unit_ends = jnp.cumsum(group_counts)
    target = lax.iota(jnp.int32, ROWS_DEV)
    passed = (target[:, None] >= unit_ends[None, :]).astype(jnp.int32)
    owner_unit = jnp.sum(passed, axis=1)
    owner_start = jnp.sum(passed * group_counts[None, :], axis=1)
    source = owner_unit * capacity + target - owner_start
    return jnp.take(panels, source, axis=0, mode="clip")


def local(unit_rows, unit_counts, seating, channel_scale):
    capacity = unit_rows.shape[2]
    group_counts = unit_counts[0]
    seated = seat_and_scale(unit_rows[0, 0], channel_scale, seating)
    panels = lax.all_to_all(seated, "pairs", 0, 0, tiled=True)
    current = compact(panels.reshape(-1, 2 * BLOCK), group_counts, capacity)
    return second_round(*advance(*first_round(current)))


def solution(mesh):
    return jax.shard_map(
        local,
        mesh=mesh,
        in_specs=(P("rows", "pairs", None, None), P("rows", None), P(), P()),
        out_specs=P("rows", "pairs"),
        check_vma=False,
    )
```

```python
import jax
import jax.numpy as jnp
from jax import lax
from jax.experimental import pallas as pl
from jax.experimental.pallas import tpu as pltpu
from jax.sharding import PartitionSpec as P

ROWS_DEV = 1024
BLOCK = 256


epsilon = 1e-06
HI = lax.Precision.HIGHEST
BIG = lax.Precision.HIGH
NEWTON_TOL_SQ = 1e-6
NEWTON_MAX = 60


def passed_along(array, axis, by):
    length = lax.axis_size(axis)
    pairs = [(i, i + by) for i in range(length) if 0 <= i + by < length]
    return lax.ppermute(array, axis, pairs)


def spd_inverse(sym_part):
    n = sym_part.shape[0]
    identity = jnp.eye(n, dtype=jnp.float32)
    bound = jnp.max(jnp.sum(jnp.abs(sym_part), axis=1))
    scale = 2.0 / (1.0 + bound)
    start = identity - scale * sym_part
    inverse = scale * (identity + start)
    residual = jnp.dot(start, start, precision=HI)
    err = jnp.sum(residual * residual)

    def cond(state):
        step, _, _, err = state
        return jnp.logical_and(err > NEWTON_TOL_SQ, step < NEWTON_MAX)

    def body(state):
        step, inverse, residual, _ = state
        inverse = inverse + jnp.dot(inverse, residual, precision=HI)
        residual = identity - jnp.dot(sym_part, inverse, precision=HI)
        return step + 1, inverse, residual, jnp.sum(residual * residual)

    def more(state):
        return lax.while_loop(cond, body, state)

    state = (jnp.int32(1), inverse, residual, err)
    _, inverse, residual, _ = lax.cond(err > NEWTON_TOL_SQ, more, lambda state: state, state)
    return inverse + jnp.dot(inverse, residual, precision=HI)


def row_sum(partial, axis):
    count = lax.axis_size(axis)
    rows, cols = partial.shape
    pieces = lax.all_to_all(partial.reshape(count, rows // count, cols), axis, 0, 0, tiled=False)
    block = jnp.sum(pieces, axis=0)
    spread = jnp.broadcast_to(block[None], (count, rows // count, cols))
    return lax.all_to_all(spread, axis, 0, 0, tiled=False).reshape(rows, cols)


def seat_kernel(seat_ref, *refs):
    count = (len(refs) - 1) // 2
    blocks, scales, out_ref = refs[:count], refs[count:2 * count], refs[-1]
    for k in range(count):
        out_ref[k // 2, :, (k % 2) * BLOCK:(k % 2 + 1) * BLOCK] = blocks[k][...] * scales[k][...]


def seat_and_scale(rows, scale, seating):
    capacity, columns = rows.shape
    pairs = columns // (2 * BLOCK)
    step_pairs = 4
    seats = 2 * step_pairs
    block_of = lambda k: (lambda q, seat: (0, seat[seats * q + k]))
    return pl.pallas_call(
        seat_kernel,
        out_shape=jax.ShapeDtypeStruct((pairs, capacity, 2 * BLOCK), jnp.float32),
        grid_spec=pltpu.PrefetchScalarGridSpec(
            num_scalar_prefetch=1,
            grid=(pairs // step_pairs,),
            in_specs=[pl.BlockSpec((capacity, BLOCK), block_of(k)) for k in range(seats)]
            + [pl.BlockSpec((1, BLOCK), block_of(k)) for k in range(seats)],
            out_specs=pl.BlockSpec((step_pairs, capacity, 2 * BLOCK), lambda q, seat: (q, 0, 0)),
        ),
    )(seating, *([rows] * seats), *([scale.reshape(1, columns)] * seats))


def row_gather_sum(partial, axis):
    count = lax.axis_size(axis)
    spread = jnp.broadcast_to(partial[None], (count,) + partial.shape)
    return jnp.sum(lax.all_to_all(spread, axis, 0, 0, tiled=False), axis=0)


def cayley(gram_full):
    identity = jnp.eye(gram_full.shape[0], dtype=jnp.float32)
    diag_terms = jnp.sum(gram_full * identity, axis=0)
    skew_part = (
        gram_full
        * (diag_terms[None, :] - diag_terms[:, None])
        / (2.0 * (diag_terms[:, None] ** 2 + diag_terms[None, :] ** 2) + epsilon)
    )
    skew_square = jnp.dot(skew_part, skew_part, precision=HI)
    numerator = identity + skew_part + 0.25 * skew_square
    sym_part = identity - 0.25 * skew_square
    return jnp.dot(numerator, spd_inverse(sym_part), precision=HI)


def first_round(panels):
    partial_gram = lax.dot_general(
        panels,
        panels,
        (((0,), (0,)), ((), ())),
        precision=BIG,
        preferred_element_type=jnp.float32,
    )
    gram_full = row_sum(partial_gram, "rows")
    rotation = cayley(gram_full)
    turned = jnp.dot(panels, rotation, precision=BIG)
    gram_turned = jnp.dot(gram_full, rotation, precision=HI)
    half_width = panels.shape[1] // 2
    block_gram = lambda cut: lax.dot_general(
        rotation[:, cut], gram_turned[:, cut], (((0,), (0,)), ((), ())), precision=HI
    )
    return turned, block_gram(slice(0, half_width)), block_gram(slice(half_width, None))


def advance(panels, upper_gram, lower_gram):
    half_width = panels.shape[1] // 2
    rows = panels.shape[0]
    upper = panels[:, :half_width]
    lower = panels[:, half_width:]
    pair_index = lax.axis_index("pairs")
    last_pair = lax.axis_size("pairs") - 1
    first = pair_index == 0
    last = pair_index == last_pair
    upward = jnp.concatenate(
        [jnp.where(first, lower, upper), jnp.where(first, lower_gram, upper_gram)], axis=0
    )
    came_up = passed_along(upward, "pairs", 1)
    came_down = passed_along(jnp.concatenate([lower, lower_gram], axis=0), "pairs", -1)
    new_upper = jnp.where(first, upper, came_up[:rows])
    new_upper_gram = jnp.where(first, upper_gram, came_up[rows:])
    new_lower = jnp.where(last, upper, came_down[:rows])
    new_lower_gram = jnp.where(last, upper_gram, came_down[rows:])
    return new_upper, new_lower, new_upper_gram, new_lower_gram


def second_round(upper, lower, upper_gram, lower_gram):
    partial_cross = lax.dot_general(
        upper,
        lower,
        (((0,), (0,)), ((), ())),
        precision=BIG,
        preferred_element_type=jnp.float32,
    )
    cross = row_gather_sum(partial_cross, "rows")
    gram_full = jnp.concatenate(
        [
            jnp.concatenate([upper_gram, cross], axis=1),
            jnp.concatenate([cross.T, lower_gram], axis=1),
        ],
        axis=0,
    )
    rotation = cayley(gram_full)
    half_width = upper.shape[1]
    return jnp.dot(upper, rotation[:half_width], precision=BIG) + jnp.dot(
        lower, rotation[half_width:], precision=BIG
    )


def compact(panels, group_counts, capacity):
    unit_ends = jnp.cumsum(group_counts)
    target = lax.iota(jnp.int32, ROWS_DEV)
    passed = (target[:, None] >= unit_ends[None, :]).astype(jnp.int32)
    owner_unit = jnp.sum(passed, axis=1)
    owner_start = jnp.sum(passed * group_counts[None, :], axis=1)
    source = owner_unit * capacity + target - owner_start
    return jnp.take(panels, source, axis=0, mode="clip")


def local(unit_rows, unit_counts, seating, channel_scale):
    capacity = unit_rows.shape[2]
    group_counts = unit_counts[0]
    seated = seat_and_scale(unit_rows[0, 0], channel_scale, seating)
    panels = lax.all_to_all(seated, "pairs", 0, 0, tiled=True)
    current = compact(panels.reshape(-1, 2 * BLOCK), group_counts, capacity)
    return second_round(*advance(*first_round(current)))


def solution(mesh):
    return jax.shard_map(
        local,
        mesh=mesh,
        in_specs=(P("rows", "pairs", None, None), P("rows", None), P(), P()),
        out_specs=P("rows", "pairs"),
        check_vma=False,
    )
```

```python
import jax
import jax.numpy as jnp
from jax import lax
from jax.experimental import pallas as pl
from jax.experimental.pallas import tpu as pltpu
from jax.sharding import PartitionSpec as P

ROWS_DEV = 1024
BLOCK = 256


epsilon = 1e-06
HI = lax.Precision.HIGHEST
BIG = lax.Precision.HIGH
NEWTON_TOL_SQ = 1e-6
NEWTON_MAX = 60


def passed_along(array, axis, by):
    length = lax.axis_size(axis)
    pairs = [(i, i + by) for i in range(length) if 0 <= i + by < length]
    return lax.ppermute(array, axis, pairs)


def spd_inverse(sym_part):
    n = sym_part.shape[0]
    identity = jnp.eye(n, dtype=jnp.float32)
    spread = jnp.sqrt(jnp.sum((sym_part - identity) ** 2))
    scale = jnp.where(spread < 1.0, 1.0, 2.0 / (2.0 + spread))
    start = identity - scale * sym_part
    inverse = scale * (identity + start)
    residual = lax.optimization_barrier(jnp.dot(start, start, precision=HI))
    err = jnp.sum(residual * residual)

    def cond(state):
        step, _, _, err = state
        return jnp.logical_and(err > NEWTON_TOL_SQ, step < NEWTON_MAX)

    def body(state):
        step, inverse, residual, _ = state
        inverse = inverse + jnp.dot(inverse, residual, precision=HI)
        residual = identity - jnp.dot(sym_part, inverse, precision=HI)
        return step + 1, inverse, residual, jnp.sum(residual * residual)

    def more(state):
        return lax.while_loop(cond, body, state)

    state = (jnp.int32(1), inverse, residual, err)
    _, inverse, residual, _ = lax.cond(err > NEWTON_TOL_SQ, more, lambda state: state, state)
    return inverse + jnp.dot(inverse, residual, precision=HI)


def row_sum(partial, axis):
    count = lax.axis_size(axis)
    rows, cols = partial.shape
    pieces = lax.all_to_all(partial.reshape(count, rows // count, cols), axis, 0, 0, tiled=False)
    block = jnp.sum(pieces, axis=0)
    spread = jnp.broadcast_to(block[None], (count, rows // count, cols))
    return lax.all_to_all(spread, axis, 0, 0, tiled=False).reshape(rows, cols)


def seat_kernel(seat_ref, *refs):
    count = (len(refs) - 1) // 2
    blocks, scales, out_ref = refs[:count], refs[count:2 * count], refs[-1]
    for k in range(count):
        out_ref[k // 2, :, (k % 2) * BLOCK:(k % 2 + 1) * BLOCK] = blocks[k][...] * scales[k][...]


def seat_and_scale(rows, scale, seating):
    capacity, columns = rows.shape
    pairs = columns // (2 * BLOCK)
    step_pairs = 4
    seats = 2 * step_pairs
    block_of = lambda k: (lambda q, seat: (0, seat[seats * q + k]))
    return pl.pallas_call(
        seat_kernel,
        out_shape=jax.ShapeDtypeStruct((pairs, capacity, 2 * BLOCK), jnp.float32),
        grid_spec=pltpu.PrefetchScalarGridSpec(
            num_scalar_prefetch=1,
            grid=(pairs // step_pairs,),
            in_specs=[pl.BlockSpec((capacity, BLOCK), block_of(k)) for k in range(seats)]
            + [pl.BlockSpec((1, BLOCK), block_of(k)) for k in range(seats)],
            out_specs=pl.BlockSpec((step_pairs, capacity, 2 * BLOCK), lambda q, seat: (q, 0, 0)),
        ),
    )(seating, *([rows] * seats), *([scale.reshape(1, columns)] * seats))


def row_gather_sum(partial, axis):
    count = lax.axis_size(axis)
    spread = jnp.broadcast_to(partial[None], (count,) + partial.shape)
    return jnp.sum(lax.all_to_all(spread, axis, 0, 0, tiled=False), axis=0)


def cayley(gram_full):
    identity = jnp.eye(gram_full.shape[0], dtype=jnp.float32)
    diag_terms = jnp.sum(gram_full * identity, axis=0)
    skew_part = (
        gram_full
        * (diag_terms[None, :] - diag_terms[:, None])
        / (2.0 * (diag_terms[:, None] ** 2 + diag_terms[None, :] ** 2) + epsilon)
    )
    skew_square = jnp.dot(skew_part, skew_part, precision=HI)
    numerator = identity + skew_part + 0.25 * skew_square
    sym_part = identity - 0.25 * skew_square
    return jnp.dot(numerator, spd_inverse(sym_part), precision=HI)


def first_round(panels):
    partial_gram = lax.dot_general(
        panels,
        panels,
        (((0,), (0,)), ((), ())),
        precision=BIG,
        preferred_element_type=jnp.float32,
    )
    gram_full = row_sum(partial_gram, "rows")
    rotation = cayley(gram_full)
    turned = jnp.dot(panels, rotation, precision=BIG)
    gram_turned = jnp.dot(gram_full, rotation, precision=HI)
    half_width = panels.shape[1] // 2
    block_gram = lambda cut: lax.dot_general(
        rotation[:, cut], gram_turned[:, cut], (((0,), (0,)), ((), ())), precision=HI
    )
    return turned, block_gram(slice(0, half_width)), block_gram(slice(half_width, None))


def advance(panels, upper_gram, lower_gram):
    half_width = panels.shape[1] // 2
    rows = panels.shape[0]
    upper = panels[:, :half_width]
    lower = panels[:, half_width:]
    pair_index = lax.axis_index("pairs")
    last_pair = lax.axis_size("pairs") - 1
    first = pair_index == 0
    last = pair_index == last_pair
    upward = jnp.concatenate(
        [jnp.where(first, lower, upper), jnp.where(first, lower_gram, upper_gram)], axis=0
    )
    came_up = passed_along(upward, "pairs", 1)
    came_down = passed_along(jnp.concatenate([lower, lower_gram], axis=0), "pairs", -1)
    new_upper = jnp.where(first, upper, came_up[:rows])
    new_upper_gram = jnp.where(first, upper_gram, came_up[rows:])
    new_lower = jnp.where(last, upper, came_down[:rows])
    new_lower_gram = jnp.where(last, upper_gram, came_down[rows:])
    return new_upper, new_lower, new_upper_gram, new_lower_gram


def second_round(upper, lower, upper_gram, lower_gram):
    partial_cross = lax.dot_general(
        upper,
        lower,
        (((0,), (0,)), ((), ())),
        precision=BIG,
        preferred_element_type=jnp.float32,
    )
    cross = row_gather_sum(partial_cross, "rows")
    gram_full = jnp.concatenate(
        [
            jnp.concatenate([upper_gram, cross], axis=1),
            jnp.concatenate([cross.T, lower_gram], axis=1),
        ],
        axis=0,
    )
    rotation = cayley(gram_full)
    half_width = upper.shape[1]
    return jnp.dot(upper, rotation[:half_width], precision=BIG) + jnp.dot(
        lower, rotation[half_width:], precision=BIG
    )


def compact(panels, group_counts, capacity):
    unit_ends = jnp.cumsum(group_counts)
    target = lax.iota(jnp.int32, ROWS_DEV)
    passed = (target[:, None] >= unit_ends[None, :]).astype(jnp.int32)
    owner_unit = jnp.sum(passed, axis=1)
    owner_start = jnp.sum(passed * group_counts[None, :], axis=1)
    source = owner_unit * capacity + target - owner_start
    return jnp.take(panels, source, axis=0, mode="clip")


def local(unit_rows, unit_counts, seating, channel_scale):
    capacity = unit_rows.shape[2]
    group_counts = unit_counts[0]
    seated = seat_and_scale(unit_rows[0, 0], channel_scale, seating)
    panels = lax.all_to_all(seated, "pairs", 0, 0, tiled=True)
    current = compact(panels.reshape(-1, 2 * BLOCK), group_counts, capacity)
    return second_round(*advance(*first_round(current)))


def solution(mesh):
    return jax.shard_map(
        local,
        mesh=mesh,
        in_specs=(P("rows", "pairs", None, None), P("rows", None), P(), P()),
        out_specs=P("rows", "pairs"),
        check_vma=False,
    )
```

```python
import jax
import jax.numpy as jnp
from jax import lax
from jax.experimental import pallas as pl
from jax.experimental.pallas import tpu as pltpu
from jax.sharding import PartitionSpec as P

ROWS_DEV = 1024
BLOCK = 256


epsilon = 1e-06
HI = lax.Precision.HIGHEST
BIG = lax.Precision.HIGH
NEWTON_TOL_SQ = 1e-6
NEWTON_MAX = 60


def passed_along(array, axis, by):
    length = lax.axis_size(axis)
    pairs = [(i, i + by) for i in range(length) if 0 <= i + by < length]
    return lax.ppermute(array, axis, pairs)


def spd_inverse(sym_part):
    n = sym_part.shape[0]
    identity = jnp.eye(n, dtype=jnp.float32)
    spread = jnp.sqrt(jnp.sum((sym_part - identity) ** 2))
    scale = jnp.where(spread < 1.0, 1.0, 2.0 / (2.0 + spread))
    start = identity - scale * sym_part
    inverse = scale * (identity + start)
    residual = lax.optimization_barrier(jnp.dot(start, start, precision=HI))
    err = jnp.sum(residual * residual)

    def cond(state):
        step, _, _, err = state
        return jnp.logical_and(err > NEWTON_TOL_SQ, step < NEWTON_MAX)

    def body(state):
        step, inverse, residual, _ = state
        inverse = inverse + jnp.dot(inverse, residual, precision=HI)
        residual = identity - jnp.dot(sym_part, inverse, precision=HI)
        return step + 1, inverse, residual, jnp.sum(residual * residual)

    def more(state):
        return lax.while_loop(cond, body, state)

    state = (jnp.int32(1), inverse, residual, err)
    _, inverse, residual, _ = lax.cond(err > NEWTON_TOL_SQ, more, lambda state: state, state)
    return inverse + jnp.dot(inverse, residual, precision=HI)


def row_sum(partial, axis):
    count = lax.axis_size(axis)
    rows, cols = partial.shape
    pieces = lax.all_to_all(partial.reshape(count, rows // count, cols), axis, 0, 0, tiled=False)
    block = jnp.sum(pieces, axis=0)
    spread = jnp.broadcast_to(block[None], (count, rows // count, cols))
    return lax.all_to_all(spread, axis, 0, 0, tiled=False).reshape(rows, cols)


def seat_kernel(seat_ref, *refs):
    count = (len(refs) - 1) // 2
    blocks, scales, out_ref = refs[:count], refs[count:2 * count], refs[-1]
    for k in range(count):
        out_ref[k // 2, :, (k % 2) * BLOCK:(k % 2 + 1) * BLOCK] = blocks[k][...] * scales[k][...]


def seat_and_scale(rows, scale, seating):
    capacity, columns = rows.shape
    pairs = columns // (2 * BLOCK)
    step_pairs = 4
    seats = 2 * step_pairs
    block_of = lambda k: (lambda q, seat: (0, seat[seats * q + k]))
    return pl.pallas_call(
        seat_kernel,
        out_shape=jax.ShapeDtypeStruct((pairs, capacity, 2 * BLOCK), jnp.float32),
        grid_spec=pltpu.PrefetchScalarGridSpec(
            num_scalar_prefetch=1,
            grid=(pairs // step_pairs,),
            in_specs=[pl.BlockSpec((capacity, BLOCK), block_of(k)) for k in range(seats)]
            + [pl.BlockSpec((1, BLOCK), block_of(k)) for k in range(seats)],
            out_specs=pl.BlockSpec((step_pairs, capacity, 2 * BLOCK), lambda q, seat: (q, 0, 0)),
        ),
    )(seating, *([rows] * seats), *([scale.reshape(1, columns)] * seats))


def row_gather_sum(partial, axis):
    count = lax.axis_size(axis)
    spread = jnp.broadcast_to(partial[None], (count,) + partial.shape)
    return jnp.sum(lax.all_to_all(spread, axis, 0, 0, tiled=False), axis=0)


def cayley(gram_full):
    identity = jnp.eye(gram_full.shape[0], dtype=jnp.float32)
    diag_terms = jnp.sum(gram_full * identity, axis=0)
    skew_part = (
        gram_full
        * (diag_terms[None, :] - diag_terms[:, None])
        / (2.0 * (diag_terms[:, None] ** 2 + diag_terms[None, :] ** 2) + epsilon)
    )
    skew_square = jnp.dot(skew_part, skew_part, precision=HI)
    numerator = identity + skew_part + 0.25 * skew_square
    sym_part = identity - 0.25 * skew_square
    return jnp.dot(numerator, spd_inverse(sym_part), precision=HI)


def first_round(panels):
    partial_gram = lax.dot_general(
        panels,
        panels,
        (((0,), (0,)), ((), ())),
        precision=BIG,
        preferred_element_type=jnp.float32,
    )
    gram_full = row_sum(partial_gram, "rows")
    return gram_full, cayley(gram_full)


def block_gram(gram_full, block):
    return lax.dot_general(
        block, jnp.dot(gram_full, block, precision=HI), (((0,), (0,)), ((), ())), precision=HI
    )


def advance(panels, gram_full, rotation):
    half_width = panels.shape[1] // 2
    pair_index = lax.axis_index("pairs")
    last_pair = lax.axis_size("pairs") - 1
    first = pair_index == 0
    last = pair_index == last_pair
    from_left = passed_along(panels, "pairs", 1)
    from_right = passed_along(panels, "pairs", -1)
    upper_cols = rotation[:, :half_width]
    lower_cols = rotation[:, half_width:]
    up_cols = jnp.where(first, lower_cols, upper_cols)
    upward = jnp.concatenate([up_cols, block_gram(gram_full, up_cols)], axis=0)
    downward = jnp.concatenate([lower_cols, block_gram(gram_full, lower_cols)], axis=0)
    came_up = passed_along(upward, "pairs", 1)
    came_down = passed_along(downward, "pairs", -1)
    rows = rotation.shape[0]
    own_upper = jnp.concatenate([upper_cols, block_gram(gram_full, upper_cols)], axis=0)
    left_msg = jnp.where(first, own_upper, came_up)
    right_msg = jnp.where(last, own_upper, came_down)
    left_panel = jnp.where(first, panels, from_left)
    right_panel = jnp.where(last, panels, from_right)
    new_upper = jnp.dot(left_panel, left_msg[:rows], precision=BIG)
    new_lower = jnp.dot(right_panel, right_msg[:rows], precision=BIG)
    return new_upper, new_lower, left_msg[rows:], right_msg[rows:]


def second_round(upper, lower, upper_gram, lower_gram):
    partial_cross = lax.dot_general(
        upper,
        lower,
        (((0,), (0,)), ((), ())),
        precision=BIG,
        preferred_element_type=jnp.float32,
    )
    cross = row_gather_sum(partial_cross, "rows")
    gram_full = jnp.concatenate(
        [
            jnp.concatenate([upper_gram, cross], axis=1),
            jnp.concatenate([cross.T, lower_gram], axis=1),
        ],
        axis=0,
    )
    rotation = cayley(gram_full)
    half_width = upper.shape[1]
    return jnp.dot(upper, rotation[:half_width], precision=BIG) + jnp.dot(
        lower, rotation[half_width:], precision=BIG
    )


def compact(panels, group_counts, capacity):
    unit_ends = jnp.cumsum(group_counts)
    target = lax.iota(jnp.int32, ROWS_DEV)
    passed = (target[:, None] >= unit_ends[None, :]).astype(jnp.int32)
    owner_unit = jnp.sum(passed, axis=1)
    owner_start = jnp.sum(passed * group_counts[None, :], axis=1)
    source = owner_unit * capacity + target - owner_start
    return jnp.take(panels, source, axis=0, mode="clip")


def local(unit_rows, unit_counts, seating, channel_scale):
    capacity = unit_rows.shape[2]
    group_counts = unit_counts[0]
    seated = seat_and_scale(unit_rows[0, 0], channel_scale, seating)
    panels = lax.all_to_all(seated, "pairs", 0, 0, tiled=True)
    current = compact(panels.reshape(-1, 2 * BLOCK), group_counts, capacity)
    return second_round(*advance(current, *first_round(current)))


def solution(mesh):
    return jax.shard_map(
        local,
        mesh=mesh,
        in_specs=(P("rows", "pairs", None, None), P("rows", None), P(), P()),
        out_specs=P("rows", "pairs"),
        check_vma=False,
    )
```

```python
import jax
import jax.numpy as jnp
from jax import lax
from jax.experimental import pallas as pl
from jax.experimental.pallas import tpu as pltpu
from jax.sharding import PartitionSpec as P

ROWS_DEV = 1024
BLOCK = 256


epsilon = 1e-06
HI = lax.Precision.HIGHEST
BIG = lax.Precision.HIGH
NEWTON_TOL_SQ = 1e-6
NEWTON_MAX = 60


def passed_along(array, axis, by):
    length = lax.axis_size(axis)
    pairs = [(i, i + by) for i in range(length) if 0 <= i + by < length]
    return lax.ppermute(array, axis, pairs)


def spd_inverse(sym_part):
    n = sym_part.shape[0]
    identity = jnp.eye(n, dtype=jnp.float32)
    spread = jnp.sqrt(jnp.sum((sym_part - identity) ** 2))
    scale = jnp.where(spread < 1.0, 1.0, 2.0 / (2.0 + spread))
    start = identity - scale * sym_part
    inverse = scale * (identity + start)
    residual = lax.optimization_barrier(jnp.dot(start, start, precision=HI))
    err = jnp.sum(residual * residual)

    def cond(state):
        step, _, _, err = state
        return jnp.logical_and(err > NEWTON_TOL_SQ, step < NEWTON_MAX)

    def body(state):
        step, inverse, residual, _ = state
        inverse = inverse + jnp.dot(inverse, residual, precision=HI)
        residual = identity - jnp.dot(sym_part, inverse, precision=HI)
        return step + 1, inverse, residual, jnp.sum(residual * residual)

    state = (jnp.int32(1), inverse, residual, err)
    _, inverse, residual, _ = lax.while_loop(cond, body, state)
    return inverse + jnp.dot(inverse, residual, precision=HI)


def row_sum(partial, axis):
    count = lax.axis_size(axis)
    rows, cols = partial.shape
    pieces = lax.all_to_all(partial.reshape(count, rows // count, cols), axis, 0, 0, tiled=False)
    block = jnp.sum(pieces, axis=0)
    spread = jnp.broadcast_to(block[None], (count, rows // count, cols))
    return lax.all_to_all(spread, axis, 0, 0, tiled=False).reshape(rows, cols)


def seat_kernel(seat_ref, *refs):
    count = (len(refs) - 1) // 2
    blocks, scales, out_ref = refs[:count], refs[count:2 * count], refs[-1]
    for k in range(count):
        out_ref[k // 2, :, (k % 2) * BLOCK:(k % 2 + 1) * BLOCK] = blocks[k][...] * scales[k][...]


def seat_and_scale(rows, scale, seating):
    capacity, columns = rows.shape
    pairs = columns // (2 * BLOCK)
    step_pairs = 4
    seats = 2 * step_pairs
    block_of = lambda k: (lambda q, seat: (0, seat[seats * q + k]))
    return pl.pallas_call(
        seat_kernel,
        out_shape=jax.ShapeDtypeStruct((pairs, capacity, 2 * BLOCK), jnp.float32),
        grid_spec=pltpu.PrefetchScalarGridSpec(
            num_scalar_prefetch=1,
            grid=(pairs // step_pairs,),
            in_specs=[pl.BlockSpec((capacity, BLOCK), block_of(k)) for k in range(seats)]
            + [pl.BlockSpec((1, BLOCK), block_of(k)) for k in range(seats)],
            out_specs=pl.BlockSpec((step_pairs, capacity, 2 * BLOCK), lambda q, seat: (q, 0, 0)),
        ),
    )(seating, *([rows] * seats), *([scale.reshape(1, columns)] * seats))


def row_gather_sum(partial, axis):
    count = lax.axis_size(axis)
    spread = jnp.broadcast_to(partial[None], (count,) + partial.shape)
    return jnp.sum(lax.all_to_all(spread, axis, 0, 0, tiled=False), axis=0)


def cayley(gram_full):
    identity = jnp.eye(gram_full.shape[0], dtype=jnp.float32)
    diag_terms = jnp.sum(gram_full * identity, axis=0)
    skew_part = (
        gram_full
        * (diag_terms[None, :] - diag_terms[:, None])
        / (2.0 * (diag_terms[:, None] ** 2 + diag_terms[None, :] ** 2) + epsilon)
    )
    skew_square = jnp.dot(skew_part, skew_part, precision=HI)
    numerator = identity + skew_part + 0.25 * skew_square
    sym_part = identity - 0.25 * skew_square
    return jnp.dot(numerator, spd_inverse(sym_part), precision=HI)


def first_round(panels):
    partial_gram = lax.dot_general(
        panels,
        panels,
        (((0,), (0,)), ((), ())),
        precision=BIG,
        preferred_element_type=jnp.float32,
    )
    gram_full = row_sum(partial_gram, "rows")
    rotation = cayley(gram_full)
    turned = jnp.dot(panels, rotation, precision=BIG)
    gram_turned = jnp.dot(gram_full, rotation, precision=HI)
    half_width = panels.shape[1] // 2
    block_gram = lambda cut: lax.dot_general(
        rotation[:, cut], gram_turned[:, cut], (((0,), (0,)), ((), ())), precision=HI
    )
    return turned, block_gram(slice(0, half_width)), block_gram(slice(half_width, None))


def advance(panels, upper_gram, lower_gram):
    half_width = panels.shape[1] // 2
    rows = panels.shape[0]
    upper = panels[:, :half_width]
    lower = panels[:, half_width:]
    pair_index = lax.axis_index("pairs")
    last_pair = lax.axis_size("pairs") - 1
    first = pair_index == 0
    last = pair_index == last_pair
    upward = jnp.concatenate(
        [jnp.where(first, lower, upper), jnp.where(first, lower_gram, upper_gram)], axis=0
    )
    came_up = passed_along(upward, "pairs", 1)
    came_down = passed_along(jnp.concatenate([lower, lower_gram], axis=0), "pairs", -1)
    new_upper = jnp.where(first, upper, came_up[:rows])
    new_upper_gram = jnp.where(first, upper_gram, came_up[rows:])
    new_lower = jnp.where(last, upper, came_down[:rows])
    new_lower_gram = jnp.where(last, upper_gram, came_down[rows:])
    return new_upper, new_lower, new_upper_gram, new_lower_gram


def second_round(upper, lower, upper_gram, lower_gram):
    partial_cross = lax.dot_general(
        upper,
        lower,
        (((0,), (0,)), ((), ())),
        precision=BIG,
        preferred_element_type=jnp.float32,
    )
    cross = row_gather_sum(partial_cross, "rows")
    gram_full = jnp.concatenate(
        [
            jnp.concatenate([upper_gram, cross], axis=1),
            jnp.concatenate([cross.T, lower_gram], axis=1),
        ],
        axis=0,
    )
    rotation = cayley(gram_full)
    half_width = upper.shape[1]
    return jnp.dot(upper, rotation[:half_width], precision=BIG) + jnp.dot(
        lower, rotation[half_width:], precision=BIG
    )


def compact(panels, group_counts, capacity):
    unit_ends = jnp.cumsum(group_counts)
    target = lax.iota(jnp.int32, ROWS_DEV)
    passed = (target[:, None] >= unit_ends[None, :]).astype(jnp.int32)
    owner_unit = jnp.sum(passed, axis=1)
    owner_start = jnp.sum(passed * group_counts[None, :], axis=1)
    source = owner_unit * capacity + target - owner_start
    return jnp.take(panels, source, axis=0, mode="clip")


def local(unit_rows, unit_counts, seating, channel_scale):
    capacity = unit_rows.shape[2]
    group_counts = unit_counts[0]
    seated = seat_and_scale(unit_rows[0, 0], channel_scale, seating)
    panels = lax.all_to_all(seated, "pairs", 0, 0, tiled=True)
    current = compact(panels.reshape(-1, 2 * BLOCK), group_counts, capacity)
    return second_round(*advance(*first_round(current)))


def solution(mesh):
    return jax.shard_map(
        local,
        mesh=mesh,
        in_specs=(P("rows", "pairs", None, None), P("rows", None), P(), P()),
        out_specs=P("rows", "pairs"),
        check_vma=False,
    )
```

```python
import jax
import jax.numpy as jnp
from jax import lax
from jax.experimental import pallas as pl
from jax.experimental.pallas import tpu as pltpu
from jax.sharding import PartitionSpec as P

ROWS_DEV = 1024
BLOCK = 256


epsilon = 1e-06
HI = lax.Precision.HIGHEST
BIG = lax.Precision.HIGH
NEWTON_TOL_SQ = 1e-6
NEWTON_MAX = 60


def passed_along(array, axis, by):
    length = lax.axis_size(axis)
    pairs = [(i, i + by) for i in range(length) if 0 <= i + by < length]
    return lax.ppermute(array, axis, pairs)


def spd_inverse(sym_part):
    n = sym_part.shape[0]
    identity = jnp.eye(n, dtype=jnp.float32)
    spread = jnp.sqrt(jnp.sum((sym_part - identity) ** 2))
    scale = jnp.where(spread < 1.0, 1.0, 2.0 / (2.0 + spread))
    start = identity - scale * sym_part
    inverse = scale * (identity + start)
    residual = lax.optimization_barrier(jnp.dot(start, start, precision=HI))
    err = jnp.sum(residual * residual)

    def cond(state):
        step, _, _, err = state
        return jnp.logical_and(err > NEWTON_TOL_SQ, step < NEWTON_MAX)

    def body(state):
        step, inverse, residual, _ = state
        inverse = inverse + jnp.dot(inverse, residual, precision=HI)
        residual = identity - jnp.dot(sym_part, inverse, precision=HI)
        return step + 1, inverse, residual, jnp.sum(residual * residual)

    state = (jnp.int32(1), inverse, residual, err)
    _, inverse, residual, _ = lax.while_loop(cond, body, state)
    return inverse + jnp.dot(inverse, residual, precision=HI)


def row_sum(partial, axis):
    count = lax.axis_size(axis)
    rows, cols = partial.shape
    pieces = lax.all_to_all(partial.reshape(count, rows // count, cols), axis, 0, 0, tiled=False)
    block = jnp.sum(pieces, axis=0)
    spread = jnp.broadcast_to(block[None], (count, rows // count, cols))
    return lax.all_to_all(spread, axis, 0, 0, tiled=False).reshape(rows, cols)


def seat_kernel(seat_ref, *refs):
    count = (len(refs) - 1) // 2
    blocks, scales, out_ref = refs[:count], refs[count:2 * count], refs[-1]
    for k in range(count):
        out_ref[k // 2, :, (k % 2) * BLOCK:(k % 2 + 1) * BLOCK] = blocks[k][...] * scales[k][...]


def seat_and_scale(rows, scale, seating):
    capacity, columns = rows.shape
    pairs = columns // (2 * BLOCK)
    step_pairs = 4
    seats = 2 * step_pairs
    block_of = lambda k: (lambda q, seat: (0, seat[seats * q + k]))
    return pl.pallas_call(
        seat_kernel,
        out_shape=jax.ShapeDtypeStruct((pairs, capacity, 2 * BLOCK), jnp.float32),
        grid_spec=pltpu.PrefetchScalarGridSpec(
            num_scalar_prefetch=1,
            grid=(pairs // step_pairs,),
            in_specs=[pl.BlockSpec((capacity, BLOCK), block_of(k)) for k in range(seats)]
            + [pl.BlockSpec((1, BLOCK), block_of(k)) for k in range(seats)],
            out_specs=pl.BlockSpec((step_pairs, capacity, 2 * BLOCK), lambda q, seat: (q, 0, 0)),
        ),
    )(seating, *([rows] * seats), *([scale.reshape(1, columns)] * seats))


def row_gather_sum(partial, axis):
    count = lax.axis_size(axis)
    spread = jnp.broadcast_to(partial[None], (count,) + partial.shape)
    return jnp.sum(lax.all_to_all(spread, axis, 0, 0, tiled=False), axis=0)


def cayley(gram_full):
    identity = jnp.eye(gram_full.shape[0], dtype=jnp.float32)
    diag_terms = jnp.sum(gram_full * identity, axis=0)
    skew_part = (
        gram_full
        * (diag_terms[None, :] - diag_terms[:, None])
        / (2.0 * (diag_terms[:, None] ** 2 + diag_terms[None, :] ** 2) + epsilon)
    )
    skew_square = jnp.dot(skew_part, skew_part, precision=HI)
    numerator = identity + skew_part + 0.25 * skew_square
    sym_part = identity - 0.25 * skew_square
    return jnp.dot(numerator, spd_inverse(sym_part), precision=HI)


def first_round(panels):
    partial_gram = lax.dot_general(
        panels,
        panels,
        (((0,), (0,)), ((), ())),
        precision=BIG,
        preferred_element_type=jnp.float32,
    )
    gram_full = row_sum(partial_gram, "rows")
    rotation = cayley(gram_full)
    turned = jnp.dot(panels, rotation, precision=BIG)
    gram_turned = jnp.dot(gram_full, rotation, precision=HI)
    half_width = panels.shape[1] // 2
    block_gram = lambda cut: lax.dot_general(
        rotation[:, cut], gram_turned[:, cut], (((0,), (0,)), ((), ())), precision=HI
    )
    return turned, block_gram(slice(0, half_width)), block_gram(slice(half_width, None))


def advance(panels, upper_gram, lower_gram):
    half_width = panels.shape[1] // 2
    upper = panels[:, :half_width]
    lower = panels[:, half_width:]
    pair_index = lax.axis_index("pairs")
    last_pair = lax.axis_size("pairs") - 1
    first = pair_index == 0
    last = pair_index == last_pair
    came_up = passed_along(jnp.where(first, lower, upper), "pairs", 1)
    came_down = passed_along(lower, "pairs", -1)
    gram_up = passed_along(jnp.where(first, lower_gram, upper_gram), "pairs", 1)
    gram_down = passed_along(lower_gram, "pairs", -1)
    new_upper = jnp.where(first, upper, came_up)
    new_upper_gram = jnp.where(first, upper_gram, gram_up)
    new_lower = jnp.where(last, upper, came_down)
    new_lower_gram = jnp.where(last, upper_gram, gram_down)
    return new_upper, new_lower, new_upper_gram, new_lower_gram


def second_round(upper, lower, upper_gram, lower_gram):
    partial_cross = lax.dot_general(
        upper,
        lower,
        (((0,), (0,)), ((), ())),
        precision=BIG,
        preferred_element_type=jnp.float32,
    )
    cross = row_gather_sum(partial_cross, "rows")
    gram_full = jnp.concatenate(
        [
            jnp.concatenate([upper_gram, cross], axis=1),
            jnp.concatenate([cross.T, lower_gram], axis=1),
        ],
        axis=0,
    )
    rotation = cayley(gram_full)
    half_width = upper.shape[1]
    return jnp.dot(upper, rotation[:half_width], precision=BIG) + jnp.dot(
        lower, rotation[half_width:], precision=BIG
    )


def compact(panels, group_counts, capacity):
    unit_ends = jnp.cumsum(group_counts)
    target = lax.iota(jnp.int32, ROWS_DEV)
    passed = (target[:, None] >= unit_ends[None, :]).astype(jnp.int32)
    owner_unit = jnp.sum(passed, axis=1)
    owner_start = jnp.sum(passed * group_counts[None, :], axis=1)
    source = owner_unit * capacity + target - owner_start
    return jnp.take(panels, source, axis=0, mode="clip")


def local(unit_rows, unit_counts, seating, channel_scale):
    capacity = unit_rows.shape[2]
    group_counts = unit_counts[0]
    seated = seat_and_scale(unit_rows[0, 0], channel_scale, seating)
    panels = lax.all_to_all(seated, "pairs", 0, 0, tiled=True)
    current = compact(panels.reshape(-1, 2 * BLOCK), group_counts, capacity)
    return second_round(*advance(*first_round(current)))


def solution(mesh):
    return jax.shard_map(
        local,
        mesh=mesh,
        in_specs=(P("rows", "pairs", None, None), P("rows", None), P(), P()),
        out_specs=P("rows", "pairs"),
        check_vma=False,
    )
```

```python
import jax
import jax.numpy as jnp
from jax import lax
from jax.experimental import pallas as pl
from jax.experimental.pallas import tpu as pltpu
from jax.sharding import PartitionSpec as P

ROWS_DEV = 1024
BLOCK = 256


epsilon = 1e-06
HI = lax.Precision.HIGHEST
BIG = lax.Precision.HIGH
NEWTON_TOL_SQ = 1e-6
NEWTON_MAX = 60


def passed_along(array, axis, by):
    length = lax.axis_size(axis)
    pairs = [(i, i + by) for i in range(length) if 0 <= i + by < length]
    return lax.ppermute(array, axis, pairs)


def spd_inverse(sym_part):
    n = sym_part.shape[0]
    identity = jnp.eye(n, dtype=jnp.float32)
    spread = jnp.sqrt(jnp.sum((sym_part - identity) ** 2))
    scale = jnp.where(spread < 1.0, 1.0, 2.0 / (2.0 + spread))
    start = identity - scale * sym_part
    inverse = scale * (identity + start)
    residual = jnp.dot(start, start, precision=HI)

    def cond(state):
        step, _, residual = state
        return jnp.logical_and(jnp.sum(residual * residual) > NEWTON_TOL_SQ, step < NEWTON_MAX)

    def body(state):
        step, inverse, residual = state
        inverse = inverse + jnp.dot(inverse, residual, precision=HI)
        residual = identity - jnp.dot(sym_part, inverse, precision=HI)
        return step + 1, inverse, residual

    state = (jnp.int32(1), inverse, residual)
    _, inverse, residual = lax.while_loop(cond, body, state)
    return inverse + jnp.dot(inverse, residual, precision=HI)


def row_sum(partial, axis):
    count = lax.axis_size(axis)
    rows, cols = partial.shape
    pieces = lax.all_to_all(partial.reshape(count, rows // count, cols), axis, 0, 0, tiled=False)
    block = jnp.sum(pieces, axis=0)
    spread = jnp.broadcast_to(block[None], (count, rows // count, cols))
    return lax.all_to_all(spread, axis, 0, 0, tiled=False).reshape(rows, cols)


def seat_kernel(seat_ref, *refs):
    count = (len(refs) - 1) // 2
    blocks, scales, out_ref = refs[:count], refs[count:2 * count], refs[-1]
    for k in range(count):
        out_ref[k // 2, :, (k % 2) * BLOCK:(k % 2 + 1) * BLOCK] = blocks[k][...] * scales[k][...]


def seat_and_scale(rows, scale, seating):
    capacity, columns = rows.shape
    pairs = columns // (2 * BLOCK)
    step_pairs = 4
    seats = 2 * step_pairs
    block_of = lambda k: (lambda q, seat: (0, seat[seats * q + k]))
    return pl.pallas_call(
        seat_kernel,
        out_shape=jax.ShapeDtypeStruct((pairs, capacity, 2 * BLOCK), jnp.float32),
        grid_spec=pltpu.PrefetchScalarGridSpec(
            num_scalar_prefetch=1,
            grid=(pairs // step_pairs,),
            in_specs=[pl.BlockSpec((capacity, BLOCK), block_of(k)) for k in range(seats)]
            + [pl.BlockSpec((1, BLOCK), block_of(k)) for k in range(seats)],
            out_specs=pl.BlockSpec((step_pairs, capacity, 2 * BLOCK), lambda q, seat: (q, 0, 0)),
        ),
    )(seating, *([rows] * seats), *([scale.reshape(1, columns)] * seats))


def row_gather_sum(partial, axis):
    count = lax.axis_size(axis)
    spread = jnp.broadcast_to(partial[None], (count,) + partial.shape)
    return jnp.sum(lax.all_to_all(spread, axis, 0, 0, tiled=False), axis=0)


def cayley(gram_full):
    identity = jnp.eye(gram_full.shape[0], dtype=jnp.float32)
    diag_terms = jnp.sum(gram_full * identity, axis=0)
    skew_part = (
        gram_full
        * (diag_terms[None, :] - diag_terms[:, None])
        / (2.0 * (diag_terms[:, None] ** 2 + diag_terms[None, :] ** 2) + epsilon)
    )
    skew_square = jnp.dot(skew_part, skew_part, precision=HI)
    numerator = identity + skew_part + 0.25 * skew_square
    sym_part = identity - 0.25 * skew_square
    return jnp.dot(numerator, spd_inverse(sym_part), precision=HI)


def first_round(panels):
    partial_gram = lax.dot_general(
        panels,
        panels,
        (((0,), (0,)), ((), ())),
        precision=BIG,
        preferred_element_type=jnp.float32,
    )
    gram_full = row_sum(partial_gram, "rows")
    rotation = cayley(gram_full)
    turned = jnp.dot(panels, rotation, precision=BIG)
    gram_turned = jnp.dot(gram_full, rotation, precision=HI)
    half_width = panels.shape[1] // 2
    block_gram = lambda cut: lax.dot_general(
        rotation[:, cut], gram_turned[:, cut], (((0,), (0,)), ((), ())), precision=HI
    )
    return turned, block_gram(slice(0, half_width)), block_gram(slice(half_width, None))


def advance(panels, upper_gram, lower_gram):
    half_width = panels.shape[1] // 2
    upper = panels[:, :half_width]
    lower = panels[:, half_width:]
    pair_index = lax.axis_index("pairs")
    last_pair = lax.axis_size("pairs") - 1
    first = pair_index == 0
    last = pair_index == last_pair
    came_up = passed_along(jnp.where(first, lower, upper), "pairs", 1)
    came_down = passed_along(lower, "pairs", -1)
    gram_up = passed_along(jnp.where(first, lower_gram, upper_gram), "pairs", 1)
    gram_down = passed_along(lower_gram, "pairs", -1)
    new_upper = jnp.where(first, upper, came_up)
    new_upper_gram = jnp.where(first, upper_gram, gram_up)
    new_lower = jnp.where(last, upper, came_down)
    new_lower_gram = jnp.where(last, upper_gram, gram_down)
    return new_upper, new_lower, new_upper_gram, new_lower_gram


def second_round(upper, lower, upper_gram, lower_gram):
    partial_cross = lax.dot_general(
        upper,
        lower,
        (((0,), (0,)), ((), ())),
        precision=BIG,
        preferred_element_type=jnp.float32,
    )
    cross = row_gather_sum(partial_cross, "rows")
    gram_full = jnp.concatenate(
        [
            jnp.concatenate([upper_gram, cross], axis=1),
            jnp.concatenate([cross.T, lower_gram], axis=1),
        ],
        axis=0,
    )
    rotation = cayley(gram_full)
    half_width = upper.shape[1]
    return jnp.dot(upper, rotation[:half_width], precision=BIG) + jnp.dot(
        lower, rotation[half_width:], precision=BIG
    )


def compact(panels, group_counts, capacity):
    unit_ends = jnp.cumsum(group_counts)
    target = lax.iota(jnp.int32, ROWS_DEV)
    passed = (target[:, None] >= unit_ends[None, :]).astype(jnp.int32)
    owner_unit = jnp.sum(passed, axis=1)
    owner_start = jnp.sum(passed * group_counts[None, :], axis=1)
    source = owner_unit * capacity + target - owner_start
    return jnp.take(panels, source, axis=0, mode="clip")


def local(unit_rows, unit_counts, seating, channel_scale):
    capacity = unit_rows.shape[2]
    group_counts = unit_counts[0]
    seated = seat_and_scale(unit_rows[0, 0], channel_scale, seating)
    panels = lax.all_to_all(seated, "pairs", 0, 0, tiled=True)
    current = compact(panels.reshape(-1, 2 * BLOCK), group_counts, capacity)
    return second_round(*advance(*first_round(current)))


def solution(mesh):
    return jax.shard_map(
        local,
        mesh=mesh,
        in_specs=(P("rows", "pairs", None, None), P("rows", None), P(), P()),
        out_specs=P("rows", "pairs"),
        check_vma=False,
    )
```

```python
import jax
import jax.numpy as jnp
from jax import lax
from jax.experimental import pallas as pl
from jax.experimental.pallas import tpu as pltpu
from jax.sharding import PartitionSpec as P

ROWS_DEV = 1024
BLOCK = 256


epsilon = 1e-06
HI = lax.Precision.HIGHEST
BIG = lax.Precision.HIGH
NEWTON_TOL_SQ = 1e-6
NEWTON_MAX = 60


def passed_along(array, axis, by):
    length = lax.axis_size(axis)
    pairs = [(i, i + by) for i in range(length) if 0 <= i + by < length]
    return lax.ppermute(array, axis, pairs)


def spd_inverse(sym_part):
    n = sym_part.shape[0]
    identity = jnp.eye(n, dtype=jnp.float32)
    spread = jnp.sqrt(jnp.sum((sym_part - identity) ** 2))
    scale = jnp.where(spread < 1.0, 1.0, 2.0 / (2.0 + spread))
    start = identity - scale * sym_part
    inverse = scale * (identity + start)
    residual = lax.optimization_barrier(jnp.dot(start, start, precision=BIG))
    err = jnp.sum(residual * residual)

    def cond(state):
        step, _, _, err = state
        return jnp.logical_and(err > NEWTON_TOL_SQ, step < NEWTON_MAX)

    def body(state):
        step, inverse, residual, _ = state
        inverse = inverse + jnp.dot(inverse, residual, precision=HI)
        residual = identity - jnp.dot(sym_part, inverse, precision=HI)
        return step + 1, inverse, residual, jnp.sum(residual * residual)

    state = (jnp.int32(1), inverse, residual, err)
    _, inverse, residual, _ = lax.while_loop(cond, body, state)
    return inverse + jnp.dot(inverse, residual, precision=BIG)


def row_sum(partial, axis):
    count = lax.axis_size(axis)
    rows, cols = partial.shape
    pieces = lax.all_to_all(partial.reshape(count, rows // count, cols), axis, 0, 0, tiled=False)
    block = jnp.sum(pieces, axis=0)
    spread = jnp.broadcast_to(block[None], (count, rows // count, cols))
    return lax.all_to_all(spread, axis, 0, 0, tiled=False).reshape(rows, cols)


def seat_kernel(seat_ref, *refs):
    count = (len(refs) - 1) // 2
    blocks, scales, out_ref = refs[:count], refs[count:2 * count], refs[-1]
    for k in range(count):
        out_ref[k // 2, :, (k % 2) * BLOCK:(k % 2 + 1) * BLOCK] = blocks[k][...] * scales[k][...]


def seat_and_scale(rows, scale, seating):
    capacity, columns = rows.shape
    pairs = columns // (2 * BLOCK)
    step_pairs = 8
    seats = 2 * step_pairs
    block_of = lambda k: (lambda q, seat: (0, seat[seats * q + k]))
    return pl.pallas_call(
        seat_kernel,
        out_shape=jax.ShapeDtypeStruct((pairs, capacity, 2 * BLOCK), jnp.float32),
        grid_spec=pltpu.PrefetchScalarGridSpec(
            num_scalar_prefetch=1,
            grid=(pairs // step_pairs,),
            in_specs=[pl.BlockSpec((capacity, BLOCK), block_of(k)) for k in range(seats)]
            + [pl.BlockSpec((1, BLOCK), block_of(k)) for k in range(seats)],
            out_specs=pl.BlockSpec((step_pairs, capacity, 2 * BLOCK), lambda q, seat: (q, 0, 0)),
        ),
    )(seating, *([rows] * seats), *([scale.reshape(1, columns)] * seats))


def row_gather_sum(partial, axis):
    count = lax.axis_size(axis)
    spread = jnp.broadcast_to(partial[None], (count,) + partial.shape)
    return jnp.sum(lax.all_to_all(spread, axis, 0, 0, tiled=False), axis=0)


def cayley(gram_full):
    identity = jnp.eye(gram_full.shape[0], dtype=jnp.float32)
    diag_terms = jnp.sum(gram_full * identity, axis=0)
    skew_part = (
        gram_full
        * (diag_terms[None, :] - diag_terms[:, None])
        / (2.0 * (diag_terms[:, None] ** 2 + diag_terms[None, :] ** 2) + epsilon)
    )
    skew_square = jnp.dot(skew_part, skew_part, precision=BIG)
    numerator = identity + skew_part + 0.25 * skew_square
    sym_part = identity - 0.25 * skew_square
    return jnp.dot(numerator, spd_inverse(sym_part), precision=HI)


def first_round(panels):
    partial_gram = lax.dot_general(
        panels,
        panels,
        (((0,), (0,)), ((), ())),
        precision=BIG,
        preferred_element_type=jnp.float32,
    )
    gram_full = row_sum(partial_gram, "rows")
    rotation = cayley(gram_full)
    turned = jnp.dot(panels, rotation, precision=BIG)
    gram_turned = jnp.dot(gram_full, rotation, precision=HI)
    half_width = panels.shape[1] // 2
    block_gram = lambda cut: lax.dot_general(
        rotation[:, cut], gram_turned[:, cut], (((0,), (0,)), ((), ())), precision=HI
    )
    return turned, block_gram(slice(0, half_width)), block_gram(slice(half_width, None))


def advance(panels, upper_gram, lower_gram):
    half_width = panels.shape[1] // 2
    upper = panels[:, :half_width]
    lower = panels[:, half_width:]
    pair_index = lax.axis_index("pairs")
    last_pair = lax.axis_size("pairs") - 1
    first = pair_index == 0
    last = pair_index == last_pair
    came_up = passed_along(jnp.where(first, lower, upper), "pairs", 1)
    came_down = passed_along(lower, "pairs", -1)
    gram_up = passed_along(jnp.where(first, lower_gram, upper_gram), "pairs", 1)
    gram_down = passed_along(lower_gram, "pairs", -1)
    new_upper = jnp.where(first, upper, came_up)
    new_upper_gram = jnp.where(first, upper_gram, gram_up)
    new_lower = jnp.where(last, upper, came_down)
    new_lower_gram = jnp.where(last, upper_gram, gram_down)
    return new_upper, new_lower, new_upper_gram, new_lower_gram


def second_round(upper, lower, upper_gram, lower_gram):
    partial_cross = lax.dot_general(
        upper,
        lower,
        (((0,), (0,)), ((), ())),
        precision=BIG,
        preferred_element_type=jnp.float32,
    )
    cross = row_gather_sum(partial_cross, "rows")
    gram_full = jnp.concatenate(
        [
            jnp.concatenate([upper_gram, cross], axis=1),
            jnp.concatenate([cross.T, lower_gram], axis=1),
        ],
        axis=0,
    )
    rotation = cayley(gram_full)
    half_width = upper.shape[1]
    return jnp.dot(upper, rotation[:half_width], precision=BIG) + jnp.dot(
        lower, rotation[half_width:], precision=BIG
    )


def compact(panels, group_counts, capacity):
    unit_ends = jnp.cumsum(group_counts)
    target = lax.iota(jnp.int32, ROWS_DEV)
    passed = (target[:, None] >= unit_ends[None, :]).astype(jnp.int32)
    owner_unit = jnp.sum(passed, axis=1)
    owner_start = jnp.sum(passed * group_counts[None, :], axis=1)
    source = owner_unit * capacity + target - owner_start
    return jnp.take(panels, source, axis=0, mode="clip")


def local(unit_rows, unit_counts, seating, channel_scale):
    capacity = unit_rows.shape[2]
    group_counts = unit_counts[0]
    seated = seat_and_scale(unit_rows[0, 0], channel_scale, seating)
    panels = lax.all_to_all(seated, "pairs", 0, 0, tiled=True)
    current = compact(panels.reshape(-1, 2 * BLOCK), group_counts, capacity)
    return second_round(*advance(*first_round(current)))


def solution(mesh):
    return jax.shard_map(
        local,
        mesh=mesh,
        in_specs=(P("rows", "pairs", None, None), P("rows", None), P(), P()),
        out_specs=P("rows", "pairs"),
        check_vma=False,
    )
```

```python
import jax
import jax.numpy as jnp
from jax import lax
from jax.experimental import pallas as pl
from jax.experimental.pallas import tpu as pltpu
from jax.sharding import PartitionSpec as P

ROWS_DEV = 1024
BLOCK = 256


epsilon = 1e-06
HI = lax.Precision.HIGHEST
BIG = lax.Precision.HIGH
NEWTON_TOL_SQ = 1e-6
NEWTON_MAX = 60


def passed_along(array, axis, by):
    length = lax.axis_size(axis)
    pairs = [(i, i + by) for i in range(length) if 0 <= i + by < length]
    return lax.ppermute(array, axis, pairs)


def spd_inverse(sym_part):
    n = sym_part.shape[0]
    identity = jnp.eye(n, dtype=jnp.float32)
    spread = jnp.sqrt(jnp.sum((sym_part - identity) ** 2))
    scale = jnp.where(spread < 1.0, 1.0, 2.0 / (2.0 + spread))
    start = identity - scale * sym_part
    inverse = scale * (identity + start)
    residual = lax.optimization_barrier(jnp.dot(start, start, precision=BIG))
    err = jnp.sum(residual * residual)

    def cond(state):
        step, _, _, err = state
        return jnp.logical_and(err > NEWTON_TOL_SQ, step < NEWTON_MAX)

    def body(state):
        step, inverse, residual, _ = state
        inverse = inverse + jnp.dot(inverse, residual, precision=HI)
        residual = identity - jnp.dot(sym_part, inverse, precision=HI)
        return step + 1, inverse, residual, jnp.sum(residual * residual)

    state = (jnp.int32(1), inverse, residual, err)
    _, inverse, residual, _ = lax.while_loop(cond, body, state)
    return inverse + jnp.dot(inverse, residual, precision=BIG)


def row_sum(partial, axis):
    count = lax.axis_size(axis)
    rows, cols = partial.shape
    pieces = lax.all_to_all(partial.reshape(count, rows // count, cols), axis, 0, 0, tiled=False)
    block = jnp.sum(pieces, axis=0)
    spread = jnp.broadcast_to(block[None], (count, rows // count, cols))
    return lax.all_to_all(spread, axis, 0, 0, tiled=False).reshape(rows, cols)


def seat_kernel(seat_ref, *refs):
    count = (len(refs) - 1) // 2
    blocks, scales, out_ref = refs[:count], refs[count:2 * count], refs[-1]
    for k in range(count):
        out_ref[k // 2, :, (k % 2) * BLOCK:(k % 2 + 1) * BLOCK] = blocks[k][...] * scales[k][...]


def seat_and_scale(rows, scale, seating):
    capacity, columns = rows.shape
    pairs = columns // (2 * BLOCK)
    step_pairs = 8
    seats = 2 * step_pairs
    block_of = lambda k: (lambda q, seat: (0, seat[seats * q + k]))
    return pl.pallas_call(
        seat_kernel,
        out_shape=jax.ShapeDtypeStruct((pairs, capacity, 2 * BLOCK), jnp.float32),
        grid_spec=pltpu.PrefetchScalarGridSpec(
            num_scalar_prefetch=1,
            grid=(pairs // step_pairs,),
            in_specs=[pl.BlockSpec((capacity, BLOCK), block_of(k)) for k in range(seats)]
            + [pl.BlockSpec((1, BLOCK), block_of(k)) for k in range(seats)],
            out_specs=pl.BlockSpec((step_pairs, capacity, 2 * BLOCK), lambda q, seat: (q, 0, 0)),
        ),
    )(seating, *([rows] * seats), *([scale.reshape(1, columns)] * seats))


def row_gather_sum(partial, axis):
    count = lax.axis_size(axis)
    spread = jnp.broadcast_to(partial[None], (count,) + partial.shape)
    return jnp.sum(lax.all_to_all(spread, axis, 0, 0, tiled=False), axis=0)


def cayley(gram_full):
    identity = jnp.eye(gram_full.shape[0], dtype=jnp.float32)
    diag_terms = jnp.sum(gram_full * identity, axis=0)
    skew_part = (
        gram_full
        * (diag_terms[None, :] - diag_terms[:, None])
        / (2.0 * (diag_terms[:, None] ** 2 + diag_terms[None, :] ** 2) + epsilon)
    )
    skew_square = jnp.dot(skew_part, skew_part, precision=BIG)
    numerator = identity + skew_part + 0.25 * skew_square
    sym_part = identity - 0.25 * skew_square
    return jnp.dot(numerator, spd_inverse(sym_part), precision=BIG)


def first_round(panels):
    partial_gram = lax.dot_general(
        panels,
        panels,
        (((0,), (0,)), ((), ())),
        precision=BIG,
        preferred_element_type=jnp.float32,
    )
    gram_full = row_sum(partial_gram, "rows")
    rotation = cayley(gram_full)
    turned = jnp.dot(panels, rotation, precision=BIG)
    gram_turned = jnp.dot(gram_full, rotation, precision=BIG)
    half_width = panels.shape[1] // 2
    block_gram = lambda cut: lax.dot_general(
        rotation[:, cut], gram_turned[:, cut], (((0,), (0,)), ((), ())), precision=BIG
    )
    return turned, block_gram(slice(0, half_width)), block_gram(slice(half_width, None))


def advance(panels, upper_gram, lower_gram):
    half_width = panels.shape[1] // 2
    upper = panels[:, :half_width]
    lower = panels[:, half_width:]
    pair_index = lax.axis_index("pairs")
    last_pair = lax.axis_size("pairs") - 1
    first = pair_index == 0
    last = pair_index == last_pair
    came_up = passed_along(jnp.where(first, lower, upper), "pairs", 1)
    came_down = passed_along(lower, "pairs", -1)
    gram_up = passed_along(jnp.where(first, lower_gram, upper_gram), "pairs", 1)
    gram_down = passed_along(lower_gram, "pairs", -1)
    new_upper = jnp.where(first, upper, came_up)
    new_upper_gram = jnp.where(first, upper_gram, gram_up)
    new_lower = jnp.where(last, upper, came_down)
    new_lower_gram = jnp.where(last, upper_gram, gram_down)
    return new_upper, new_lower, new_upper_gram, new_lower_gram


def second_round(upper, lower, upper_gram, lower_gram):
    partial_cross = lax.dot_general(
        upper,
        lower,
        (((0,), (0,)), ((), ())),
        precision=BIG,
        preferred_element_type=jnp.float32,
    )
    cross = row_gather_sum(partial_cross, "rows")
    gram_full = jnp.concatenate(
        [
            jnp.concatenate([upper_gram, cross], axis=1),
            jnp.concatenate([cross.T, lower_gram], axis=1),
        ],
        axis=0,
    )
    rotation = cayley(gram_full)
    half_width = upper.shape[1]
    return jnp.dot(upper, rotation[:half_width], precision=BIG) + jnp.dot(
        lower, rotation[half_width:], precision=BIG
    )


def compact(panels, group_counts, capacity):
    unit_ends = jnp.cumsum(group_counts)
    target = lax.iota(jnp.int32, ROWS_DEV)
    passed = (target[:, None] >= unit_ends[None, :]).astype(jnp.int32)
    owner_unit = jnp.sum(passed, axis=1)
    owner_start = jnp.sum(passed * group_counts[None, :], axis=1)
    source = owner_unit * capacity + target - owner_start
    return jnp.take(panels, source, axis=0, mode="clip")


def local(unit_rows, unit_counts, seating, channel_scale):
    capacity = unit_rows.shape[2]
    group_counts = unit_counts[0]
    seated = seat_and_scale(unit_rows[0, 0], channel_scale, seating)
    panels = lax.all_to_all(seated, "pairs", 0, 0, tiled=True)
    current = compact(panels.reshape(-1, 2 * BLOCK), group_counts, capacity)
    return second_round(*advance(*first_round(current)))


def solution(mesh):
    return jax.shard_map(
        local,
        mesh=mesh,
        in_specs=(P("rows", "pairs", None, None), P("rows", None), P(), P()),
        out_specs=P("rows", "pairs"),
        check_vma=False,
    )
```

```python
import jax
import jax.numpy as jnp
from jax import lax
from jax.experimental import pallas as pl
from jax.experimental.pallas import tpu as pltpu
from jax.sharding import PartitionSpec as P

ROWS_DEV = 1024
BLOCK = 256


epsilon = 1e-06
HI = lax.Precision.HIGHEST
BIG = lax.Precision.HIGH
NEWTON_TOL_SQ = 1e-6
NEWTON_MAX = 60


def passed_along(array, axis, by):
    length = lax.axis_size(axis)
    pairs = [(i, i + by) for i in range(length) if 0 <= i + by < length]
    return lax.ppermute(array, axis, pairs)


def spd_inverse(sym_part):
    n = sym_part.shape[0]
    identity = jnp.eye(n, dtype=jnp.float32)
    spread = jnp.sqrt(jnp.sum((sym_part - identity) ** 2))
    scale = jnp.where(spread < 1.0, 1.0, 2.0 / (2.0 + spread))
    start = identity - scale * sym_part
    inverse = scale * (identity + start)
    residual = lax.optimization_barrier(jnp.dot(start, start, precision=BIG))
    err = jnp.sum(residual * residual)

    def cond(state):
        step, _, _, err = state
        return jnp.logical_and(err > NEWTON_TOL_SQ, step < NEWTON_MAX)

    def body(state):
        step, inverse, residual, _ = state
        inverse = inverse + jnp.dot(inverse, residual, precision=BIG)
        residual = identity - jnp.dot(sym_part, inverse, precision=HI)
        return step + 1, inverse, residual, jnp.sum(residual * residual)

    state = (jnp.int32(1), inverse, residual, err)
    _, inverse, residual, _ = lax.while_loop(cond, body, state)
    return inverse + jnp.dot(inverse, residual, precision=BIG)


def row_sum(partial, axis):
    count = lax.axis_size(axis)
    rows, cols = partial.shape
    pieces = lax.all_to_all(partial.reshape(count, rows // count, cols), axis, 0, 0, tiled=False)
    block = jnp.sum(pieces, axis=0)
    spread = jnp.broadcast_to(block[None], (count, rows // count, cols))
    return lax.all_to_all(spread, axis, 0, 0, tiled=False).reshape(rows, cols)


def seat_kernel(seat_ref, *refs):
    count = (len(refs) - 1) // 2
    blocks, scales, out_ref = refs[:count], refs[count:2 * count], refs[-1]
    for k in range(count):
        out_ref[k // 2, :, (k % 2) * BLOCK:(k % 2 + 1) * BLOCK] = blocks[k][...] * scales[k][...]


def seat_and_scale(rows, scale, seating):
    capacity, columns = rows.shape
    pairs = columns // (2 * BLOCK)
    step_pairs = 8
    seats = 2 * step_pairs
    block_of = lambda k: (lambda q, seat: (0, seat[seats * q + k]))
    return pl.pallas_call(
        seat_kernel,
        out_shape=jax.ShapeDtypeStruct((pairs, capacity, 2 * BLOCK), jnp.float32),
        grid_spec=pltpu.PrefetchScalarGridSpec(
            num_scalar_prefetch=1,
            grid=(pairs // step_pairs,),
            in_specs=[pl.BlockSpec((capacity, BLOCK), block_of(k)) for k in range(seats)]
            + [pl.BlockSpec((1, BLOCK), block_of(k)) for k in range(seats)],
            out_specs=pl.BlockSpec((step_pairs, capacity, 2 * BLOCK), lambda q, seat: (q, 0, 0)),
        ),
    )(seating, *([rows] * seats), *([scale.reshape(1, columns)] * seats))


def row_gather_sum(partial, axis):
    count = lax.axis_size(axis)
    spread = jnp.broadcast_to(partial[None], (count,) + partial.shape)
    return jnp.sum(lax.all_to_all(spread, axis, 0, 0, tiled=False), axis=0)


def cayley(gram_full):
    identity = jnp.eye(gram_full.shape[0], dtype=jnp.float32)
    diag_terms = jnp.sum(gram_full * identity, axis=0)
    skew_part = (
        gram_full
        * (diag_terms[None, :] - diag_terms[:, None])
        / (2.0 * (diag_terms[:, None] ** 2 + diag_terms[None, :] ** 2) + epsilon)
    )
    skew_square = jnp.dot(skew_part, skew_part, precision=BIG)
    numerator = identity + skew_part + 0.25 * skew_square
    sym_part = identity - 0.25 * skew_square
    return jnp.dot(numerator, spd_inverse(sym_part), precision=HI)


def first_round(panels):
    partial_gram = lax.dot_general(
        panels,
        panels,
        (((0,), (0,)), ((), ())),
        precision=BIG,
        preferred_element_type=jnp.float32,
    )
    gram_full = row_sum(partial_gram, "rows")
    rotation = cayley(gram_full)
    turned = jnp.dot(panels, rotation, precision=BIG)
    gram_turned = jnp.dot(gram_full, rotation, precision=BIG)
    half_width = panels.shape[1] // 2
    block_gram = lambda cut: lax.dot_general(
        rotation[:, cut], gram_turned[:, cut], (((0,), (0,)), ((), ())), precision=BIG
    )
    return turned, block_gram(slice(0, half_width)), block_gram(slice(half_width, None))


def advance(panels, upper_gram, lower_gram):
    half_width = panels.shape[1] // 2
    upper = panels[:, :half_width]
    lower = panels[:, half_width:]
    pair_index = lax.axis_index("pairs")
    last_pair = lax.axis_size("pairs") - 1
    first = pair_index == 0
    last = pair_index == last_pair
    came_up = passed_along(jnp.where(first, lower, upper), "pairs", 1)
    came_down = passed_along(lower, "pairs", -1)
    gram_up = passed_along(jnp.where(first, lower_gram, upper_gram), "pairs", 1)
    gram_down = passed_along(lower_gram, "pairs", -1)
    new_upper = jnp.where(first, upper, came_up)
    new_upper_gram = jnp.where(first, upper_gram, gram_up)
    new_lower = jnp.where(last, upper, came_down)
    new_lower_gram = jnp.where(last, upper_gram, gram_down)
    return new_upper, new_lower, new_upper_gram, new_lower_gram


def second_round(upper, lower, upper_gram, lower_gram):
    partial_cross = lax.dot_general(
        upper,
        lower,
        (((0,), (0,)), ((), ())),
        precision=BIG,
        preferred_element_type=jnp.float32,
    )
    cross = row_gather_sum(partial_cross, "rows")
    gram_full = jnp.concatenate(
        [
            jnp.concatenate([upper_gram, cross], axis=1),
            jnp.concatenate([cross.T, lower_gram], axis=1),
        ],
        axis=0,
    )
    rotation = cayley(gram_full)
    half_width = upper.shape[1]
    return jnp.dot(upper, rotation[:half_width], precision=BIG) + jnp.dot(
        lower, rotation[half_width:], precision=BIG
    )


def compact(panels, group_counts, capacity):
    unit_ends = jnp.cumsum(group_counts)
    target = lax.iota(jnp.int32, ROWS_DEV)
    passed = (target[:, None] >= unit_ends[None, :]).astype(jnp.int32)
    owner_unit = jnp.sum(passed, axis=1)
    owner_start = jnp.sum(passed * group_counts[None, :], axis=1)
    source = owner_unit * capacity + target - owner_start
    return jnp.take(panels, source, axis=0, mode="clip")


def local(unit_rows, unit_counts, seating, channel_scale):
    capacity = unit_rows.shape[2]
    group_counts = unit_counts[0]
    seated = seat_and_scale(unit_rows[0, 0], channel_scale, seating)
    panels = lax.all_to_all(seated, "pairs", 0, 0, tiled=True)
    current = compact(panels.reshape(-1, 2 * BLOCK), group_counts, capacity)
    return second_round(*advance(*first_round(current)))


def solution(mesh):
    return jax.shard_map(
        local,
        mesh=mesh,
        in_specs=(P("rows", "pairs", None, None), P("rows", None), P(), P()),
        out_specs=P("rows", "pairs"),
        check_vma=False,
    )
```

```python
import jax
import jax.numpy as jnp
from jax import lax
from jax.experimental import pallas as pl
from jax.experimental.pallas import tpu as pltpu
from jax.sharding import PartitionSpec as P

ROWS_DEV = 1024
BLOCK = 256


epsilon = 1e-06
HI = lax.Precision.HIGHEST
BIG = lax.Precision.HIGH
NEWTON_TOL_SQ = 1e-6
NEWTON_MAX = 60


def passed_along(array, axis, by):
    length = lax.axis_size(axis)
    pairs = [(i, i + by) for i in range(length) if 0 <= i + by < length]
    return lax.ppermute(array, axis, pairs)


def spd_inverse(sym_part):
    n = sym_part.shape[0]
    identity = jnp.eye(n, dtype=jnp.float32)
    spread = jnp.sqrt(jnp.sum((sym_part - identity) ** 2))
    scale = jnp.where(spread < 1.0, 1.0, 2.0 / (2.0 + spread))
    start = identity - scale * sym_part
    inverse = scale * (identity + start)
    residual = lax.optimization_barrier(jnp.dot(start, start, precision=BIG))
    err = jnp.sum(residual * residual)

    def cond(state):
        step, _, _, err = state
        return jnp.logical_and(err > NEWTON_TOL_SQ, step < NEWTON_MAX)

    def body(state):
        step, inverse, residual, _ = state
        inverse = inverse + jnp.dot(inverse, residual, precision=BIG)
        residual = identity - jnp.dot(sym_part, inverse, precision=HI)
        return step + 1, inverse, residual, jnp.sum(residual * residual)

    state = (jnp.int32(1), inverse, residual, err)
    _, inverse, residual, _ = lax.while_loop(cond, body, state)
    return inverse + jnp.dot(inverse, residual, precision=BIG)


def row_sum(partial, axis):
    count = lax.axis_size(axis)
    rows, cols = partial.shape
    pieces = lax.all_to_all(partial.reshape(count, rows // count, cols), axis, 0, 0, tiled=False)
    block = jnp.sum(pieces, axis=0)
    spread = jnp.broadcast_to(block[None], (count, rows // count, cols))
    return lax.all_to_all(spread, axis, 0, 0, tiled=False).reshape(rows, cols)


def seat_kernel(seat_ref, *refs):
    count = (len(refs) - 1) // 2
    blocks, scales, out_ref = refs[:count], refs[count:2 * count], refs[-1]
    for k in range(count):
        out_ref[k // 2, :, (k % 2) * BLOCK:(k % 2 + 1) * BLOCK] = blocks[k][...] * scales[k][...]


def seat_and_scale(rows, scale, seating):
    capacity, columns = rows.shape
    pairs = columns // (2 * BLOCK)
    step_pairs = 8
    seats = 2 * step_pairs
    block_of = lambda k: (lambda q, seat: (0, seat[seats * q + k]))
    return pl.pallas_call(
        seat_kernel,
        out_shape=jax.ShapeDtypeStruct((pairs, capacity, 2 * BLOCK), jnp.float32),
        grid_spec=pltpu.PrefetchScalarGridSpec(
            num_scalar_prefetch=1,
            grid=(pairs // step_pairs,),
            in_specs=[pl.BlockSpec((capacity, BLOCK), block_of(k)) for k in range(seats)]
            + [pl.BlockSpec((1, BLOCK), block_of(k)) for k in range(seats)],
            out_specs=pl.BlockSpec((step_pairs, capacity, 2 * BLOCK), lambda q, seat: (q, 0, 0)),
        ),
    )(seating, *([rows] * seats), *([scale.reshape(1, columns)] * seats))


def row_gather_sum(partial, axis):
    count = lax.axis_size(axis)
    spread = jnp.broadcast_to(partial[None], (count,) + partial.shape)
    return jnp.sum(lax.all_to_all(spread, axis, 0, 0, tiled=False), axis=0)


def cayley(gram_full):
    identity = jnp.eye(gram_full.shape[0], dtype=jnp.float32)
    diag_terms = jnp.sum(gram_full * identity, axis=0)
    skew_part = (
        gram_full
        * (diag_terms[None, :] - diag_terms[:, None])
        / (2.0 * (diag_terms[:, None] ** 2 + diag_terms[None, :] ** 2) + epsilon)
    )
    skew_square = jnp.dot(skew_part, skew_part, precision=BIG)
    numerator = identity + skew_part + 0.25 * skew_square
    sym_part = identity - 0.25 * skew_square
    return jnp.dot(numerator, spd_inverse(sym_part), precision=HI)


def first_round(panels):
    partial_gram = lax.dot_general(
        panels,
        panels,
        (((0,), (0,)), ((), ())),
        precision=BIG,
        preferred_element_type=jnp.float32,
    )
    gram_full = row_sum(partial_gram, "rows")
    rotation = cayley(gram_full)
    half_width = panels.shape[1] // 2
    turned_lower = jnp.dot(panels, rotation[:, half_width:], precision=BIG)
    turned_upper = jnp.dot(panels, rotation[:, :half_width], precision=BIG)
    gram_turned = jnp.dot(gram_full, rotation, precision=BIG)
    block_gram = lambda cut: lax.dot_general(
        rotation[:, cut], gram_turned[:, cut], (((0,), (0,)), ((), ())), precision=BIG
    )
    return (
        turned_upper,
        turned_lower,
        block_gram(slice(0, half_width)),
        block_gram(slice(half_width, None)),
    )


def advance(upper, lower, upper_gram, lower_gram):
    pair_index = lax.axis_index("pairs")
    last_pair = lax.axis_size("pairs") - 1
    first = pair_index == 0
    last = pair_index == last_pair
    came_up = passed_along(jnp.where(first, lower, upper), "pairs", 1)
    came_down = passed_along(lower, "pairs", -1)
    gram_up = passed_along(jnp.where(first, lower_gram, upper_gram), "pairs", 1)
    gram_down = passed_along(lower_gram, "pairs", -1)
    new_upper = jnp.where(first, upper, came_up)
    new_upper_gram = jnp.where(first, upper_gram, gram_up)
    new_lower = jnp.where(last, upper, came_down)
    new_lower_gram = jnp.where(last, upper_gram, gram_down)
    return new_upper, new_lower, new_upper_gram, new_lower_gram


def second_round(upper, lower, upper_gram, lower_gram):
    partial_cross = lax.dot_general(
        upper,
        lower,
        (((0,), (0,)), ((), ())),
        precision=BIG,
        preferred_element_type=jnp.float32,
    )
    cross = row_gather_sum(partial_cross, "rows")
    gram_full = jnp.concatenate(
        [
            jnp.concatenate([upper_gram, cross], axis=1),
            jnp.concatenate([cross.T, lower_gram], axis=1),
        ],
        axis=0,
    )
    rotation = cayley(gram_full)
    half_width = upper.shape[1]
    return jnp.dot(upper, rotation[:half_width], precision=BIG) + jnp.dot(
        lower, rotation[half_width:], precision=BIG
    )


def compact(panels, group_counts, capacity):
    unit_ends = jnp.cumsum(group_counts)
    target = lax.iota(jnp.int32, ROWS_DEV)
    passed = (target[:, None] >= unit_ends[None, :]).astype(jnp.int32)
    owner_unit = jnp.sum(passed, axis=1)
    owner_start = jnp.sum(passed * group_counts[None, :], axis=1)
    source = owner_unit * capacity + target - owner_start
    return jnp.take(panels, source, axis=0, mode="clip")


def local(unit_rows, unit_counts, seating, channel_scale):
    capacity = unit_rows.shape[2]
    group_counts = unit_counts[0]
    seated = seat_and_scale(unit_rows[0, 0], channel_scale, seating)
    panels = lax.all_to_all(seated, "pairs", 0, 0, tiled=True)
    current = compact(panels.reshape(-1, 2 * BLOCK), group_counts, capacity)
    return second_round(*advance(*first_round(current)))


def solution(mesh):
    return jax.shard_map(
        local,
        mesh=mesh,
        in_specs=(P("rows", "pairs", None, None), P("rows", None), P(), P()),
        out_specs=P("rows", "pairs"),
        check_vma=False,
    )
```

```python
import jax
import jax.numpy as jnp
from jax import lax
from jax.experimental import pallas as pl
from jax.experimental.pallas import tpu as pltpu
from jax.sharding import PartitionSpec as P

ROWS_DEV = 1024
BLOCK = 256


epsilon = 1e-06
HI = lax.Precision.HIGHEST
BIG = lax.Precision.HIGH
NEWTON_TOL_SQ = 1e-6
NEWTON_MAX = 60


def passed_along(array, axis, by):
    length = lax.axis_size(axis)
    pairs = [(i, i + by) for i in range(length) if 0 <= i + by < length]
    return lax.ppermute(array, axis, pairs)


def spd_inverse(sym_part):
    n = sym_part.shape[0]
    identity = jnp.eye(n, dtype=jnp.float32)
    spread = jnp.sqrt(jnp.sum((sym_part - identity) ** 2))
    scale = jnp.where(spread < 1.0, 1.0, 2.0 / (2.0 + spread))
    start = identity - scale * sym_part
    inverse = scale * (identity + start)
    residual = jnp.dot(start, start, precision=BIG)
    err = jnp.sum(residual * residual)

    def cond(state):
        step, _, _, err = state
        return jnp.logical_and(err > NEWTON_TOL_SQ, step < NEWTON_MAX)

    def body(state):
        step, inverse, residual, _ = state
        inverse = inverse + jnp.dot(inverse, residual, precision=BIG)
        residual = identity - jnp.dot(sym_part, inverse, precision=HI)
        return step + 1, inverse, residual, jnp.sum(residual * residual)

    state = (jnp.int32(1), inverse, residual, err)
    _, inverse, residual, _ = lax.while_loop(cond, body, state)
    return inverse + jnp.dot(inverse, residual, precision=BIG)


def row_sum(partial, axis):
    count = lax.axis_size(axis)
    rows, cols = partial.shape
    pieces = lax.all_to_all(partial.reshape(count, rows // count, cols), axis, 0, 0, tiled=False)
    block = jnp.sum(pieces, axis=0)
    spread = jnp.broadcast_to(block[None], (count, rows // count, cols))
    return lax.all_to_all(spread, axis, 0, 0, tiled=False).reshape(rows, cols)


def seat_kernel(seat_ref, *refs):
    count = (len(refs) - 1) // 2
    blocks, scales, out_ref = refs[:count], refs[count:2 * count], refs[-1]
    for k in range(count):
        out_ref[k // 2, :, (k % 2) * BLOCK:(k % 2 + 1) * BLOCK] = blocks[k][...] * scales[k][...]


def seat_and_scale(rows, scale, seating):
    capacity, columns = rows.shape
    pairs = columns // (2 * BLOCK)
    step_pairs = 8
    seats = 2 * step_pairs
    block_of = lambda k: (lambda q, seat: (0, seat[seats * q + k]))
    return pl.pallas_call(
        seat_kernel,
        out_shape=jax.ShapeDtypeStruct((pairs, capacity, 2 * BLOCK), jnp.float32),
        grid_spec=pltpu.PrefetchScalarGridSpec(
            num_scalar_prefetch=1,
            grid=(pairs // step_pairs,),
            in_specs=[pl.BlockSpec((capacity, BLOCK), block_of(k)) for k in range(seats)]
            + [pl.BlockSpec((1, BLOCK), block_of(k)) for k in range(seats)],
            out_specs=pl.BlockSpec((step_pairs, capacity, 2 * BLOCK), lambda q, seat: (q, 0, 0)),
        ),
    )(seating, *([rows] * seats), *([scale.reshape(1, columns)] * seats))


def row_gather_sum(partial, axis):
    count = lax.axis_size(axis)
    spread = jnp.broadcast_to(partial[None], (count,) + partial.shape)
    return jnp.sum(lax.all_to_all(spread, axis, 0, 0, tiled=False), axis=0)


def cayley(gram_full):
    identity = jnp.eye(gram_full.shape[0], dtype=jnp.float32)
    diag_terms = jnp.sum(gram_full * identity, axis=0)
    skew_part = (
        gram_full
        * (diag_terms[None, :] - diag_terms[:, None])
        / (2.0 * (diag_terms[:, None] ** 2 + diag_terms[None, :] ** 2) + epsilon)
    )
    skew_square = jnp.dot(skew_part, skew_part, precision=BIG)
    numerator = identity + skew_part + 0.25 * skew_square
    sym_part = identity - 0.25 * skew_square
    return jnp.dot(numerator, spd_inverse(sym_part), precision=HI)


def first_round(panels):
    partial_gram = lax.dot_general(
        panels,
        panels,
        (((0,), (0,)), ((), ())),
        precision=BIG,
        preferred_element_type=jnp.float32,
    )
    gram_full = row_sum(partial_gram, "rows")
    rotation = cayley(gram_full)
    turned = jnp.dot(panels, rotation, precision=BIG)
    gram_turned = jnp.dot(gram_full, rotation, precision=BIG)
    half_width = panels.shape[1] // 2
    block_gram = lambda cut: lax.dot_general(
        rotation[:, cut], gram_turned[:, cut], (((0,), (0,)), ((), ())), precision=BIG
    )
    return turned, block_gram(slice(0, half_width)), block_gram(slice(half_width, None))


def advance(panels, upper_gram, lower_gram):
    half_width = panels.shape[1] // 2
    upper = panels[:, :half_width]
    lower = panels[:, half_width:]
    pair_index = lax.axis_index("pairs")
    last_pair = lax.axis_size("pairs") - 1
    first = pair_index == 0
    last = pair_index == last_pair
    came_up = passed_along(jnp.where(first, lower, upper), "pairs", 1)
    came_down = passed_along(lower, "pairs", -1)
    gram_up = passed_along(jnp.where(first, lower_gram, upper_gram), "pairs", 1)
    gram_down = passed_along(lower_gram, "pairs", -1)
    new_upper = jnp.where(first, upper, came_up)
    new_upper_gram = jnp.where(first, upper_gram, gram_up)
    new_lower = jnp.where(last, upper, came_down)
    new_lower_gram = jnp.where(last, upper_gram, gram_down)
    return new_upper, new_lower, new_upper_gram, new_lower_gram


def second_round(upper, lower, upper_gram, lower_gram):
    partial_cross = lax.dot_general(
        upper,
        lower,
        (((0,), (0,)), ((), ())),
        precision=BIG,
        preferred_element_type=jnp.float32,
    )
    cross = row_gather_sum(partial_cross, "rows")
    gram_full = jnp.concatenate(
        [
            jnp.concatenate([upper_gram, cross], axis=1),
            jnp.concatenate([cross.T, lower_gram], axis=1),
        ],
        axis=0,
    )
    rotation = cayley(gram_full)
    half_width = upper.shape[1]
    return jnp.dot(upper, rotation[:half_width], precision=BIG) + jnp.dot(
        lower, rotation[half_width:], precision=BIG
    )


def compact(panels, group_counts, capacity):
    unit_ends = jnp.cumsum(group_counts)
    target = lax.iota(jnp.int32, ROWS_DEV)
    passed = (target[:, None] >= unit_ends[None, :]).astype(jnp.int32)
    owner_unit = jnp.sum(passed, axis=1)
    owner_start = jnp.sum(passed * group_counts[None, :], axis=1)
    source = owner_unit * capacity + target - owner_start
    return jnp.take(panels, source, axis=0, mode="clip")


def local(unit_rows, unit_counts, seating, channel_scale):
    capacity = unit_rows.shape[2]
    group_counts = unit_counts[0]
    seated = seat_and_scale(unit_rows[0, 0], channel_scale, seating)
    panels = lax.all_to_all(seated, "pairs", 0, 0, tiled=True)
    current = compact(panels.reshape(-1, 2 * BLOCK), group_counts, capacity)
    return second_round(*advance(*first_round(current)))


def solution(mesh):
    return jax.shard_map(
        local,
        mesh=mesh,
        in_specs=(P("rows", "pairs", None, None), P("rows", None), P(), P()),
        out_specs=P("rows", "pairs"),
        check_vma=False,
    )
```
